128 devices in a mesh: lon: 16 (over y, z_hi, core), lat: 8 (over x, z_lo).
Axes of the slice: x: 4, y: 4, z: 4 (z_hi: 2, z_lo: 2; z = z_hi * 2 + z_lo), core: 2. Of those that a mesh axis runs over, the one named last changes fastest.
Arguments:
- innovations: float32 [150, 65536], P(None, ('lon', 'lat')), may hold values from -6 to 6
- owner_tile: int32 [65536, 1], P(('lon', 'lat')), may hold values from 0 to 127; in each aligned block of 512 rows (0 to 511, 512 to 1023, ...) at most 16 rows name the same one
- obs_column: int32 [65536], P(('lon', 'lat')), may hold values from 0 to 8191
- obs_depth: int32 [65536], P(('lon', 'lat')), may hold values from 1 to 75
- coefficients: float32 [9, 512, 2048], P(None, 'lat', 'lon'), may hold values from 0.03 to 0.25
- sea_depth: int32 [512, 2048], P('lat', 'lon'), may hold values from 0 to 75
- balance: float32 [150, 150], replicated, may hold values from -0.5 to 0.5
Outputs:
- gradient: float32 [150, 512, 2048], P(None, 'lat', 'lon')
The draws below stay inside these ranges and needn't reach their ends.
Inputs may be any that keep to these rules, and one draw needn't show every extreme that they name: `owner_tile`: among the 512 profiles of one device, at most 16 share one owner tile, and some device holds exactly 16 for one owner.
All inputs are finite; a program needn't handle non-finite values.
Results may differ from the reference program's by a relative error of at most 0.00012.
Values sent between devices are 32-bit elements; how exact they have to be, the bound alone decides.
No kernel may reach another device: no remote copies, remote signals or barrier semaphores. Data moves between devices by JAX's collectives and lax.ppermute only.
A program may use at most 128 MiB of HBM per device.

```python
import math
import jax
import jax.numpy as jnp
import numpy as np
from jax import lax

LEVELS = 75
CH = 150
CY = 64
CX = 128
OBS_DEV = 512
PASSES = 4
NY = 512
NX = 2048
TOTAL_OBS = 65536
CAP = 16
N_LON = 16
N_LAT = 8


def plant(drawn, key, least, largest):
    longest = drawn.shape.index(max(drawn.shape))
    spots = []
    for shift in (0, 1):
        where = [jax.random.randint(jax.random.fold_in(key, axis), (), 0, length) for axis, length in enumerate(drawn.shape)]
        where[longest] = (where[longest] + shift) % drawn.shape[longest]
        spots.append(tuple(where))
    return drawn.at[spots[0]].set(least).at[spots[1]].set(largest)


def shard_levels(stream_key, extent, split, low, largest):
    factor_of, own = 1.0, jax.random.fold_in(stream_key, 6)
    for position, shards_of in split:
        draws = jnp.exp(jax.random.uniform(jax.random.fold_in(own, position), (shards_of,), jnp.float32, low / len(split), largest / len(split)))
        factor_of = factor_of * jnp.repeat(draws, extent[position] // shards_of).reshape([-1 if axis == position else 1 for axis in range(len(extent))])
    return factor_of


def shared_out(stream_key, own, number, rows, count, top, bound, slope):
    order = jax.random.permutation(stream_key, count)
    crowded, usual = shares(count, rows * top, bound, slope, True), shares(count, rows * top, bound, slope, False)
    places = jnp.arange(count)

    def named(lengths, turn):
        used = int((lengths > 0).sum())
        fixed = max(1, used // 4)
        moved = fixed + (places - fixed + turn * (used - fixed)) % max(1, count - fixed)
        return jnp.zeros((count,), jnp.int32).at[order[jnp.where(places < fixed, places, moved)]].set(jnp.asarray(lengths, jnp.int32))

    lengths = jnp.where(number % 4 == 0, named(crowded, number // 4), named(usual, number - number // 4 - 1))
    mixed = jax.random.permutation(jax.random.fold_in(own, 3), count)
    source_of, receiver = mixed[0:count // 2 * 2:2], mixed[1:count // 2 * 2:2]
    margin = jnp.minimum(lengths[source_of] - 1, bound - lengths[receiver]) // 2
    margin = jnp.where((source_of == order[0]) | (receiver == order[0]) | (lengths[receiver] == 0), 0, jnp.maximum(margin, 0))
    moved = jax.random.randint(jax.random.fold_in(own, 4), (count // 2,), 0, 1 << 20) % (margin + 1)
    lengths = lengths.at[source_of].add(-moved).at[receiver].add(moved)
    members = jnp.searchsorted(jnp.cumsum(lengths), jnp.arange(rows * top), side="right").astype(jnp.int32)
    grid = members.reshape(top, rows).T
    grid = grid[jax.random.permutation(jax.random.fold_in(own, 1), rows)]
    turn = jax.random.randint(jax.random.fold_in(own, 2), (rows, 1), 0, top)
    return jnp.take_along_axis(grid, (jnp.arange(top)[None, :] + turn) % top, axis=1)


def shares(number_of, total, limit, skew, full):
    portions = [(1 << 20) // math.isqrt(standing ** skew) + 1 for standing in range(1, number_of + 1)]
    largest = limit if full else min(limit, max(-(-total // number_of), total * portions[0] // sum(portions)))
    least = 1 if total - largest >= number_of - 1 else 0
    given, spare = [largest] + [least] * (number_of - 1), total - largest - least * (number_of - 1)
    while spare > 0:
        free = [i for i in range(1, number_of) if given[i] < largest] or [i for i in range(1, number_of) if given[i] < limit]
        whole, remaining = sum([portions[i] for i in free]), spare
        for i in free:
            extra = min(limit - given[i], max(1, remaining * portions[i] // whole), spare)
            given[i] = given[i] + extra
            spare = spare - extra
    return np.array(given)


def centred(key, dims, scale, bound, split=(), kind=jnp.bfloat16):
    entries = jax.random.normal(key, dims, jnp.float32) * scale
    if len(split) > 0:
        entries = shard_levels(key, dims, split, -0.22, 0.18) * entries
    return jnp.clip(entries, min=-bound, max=bound).astype(kind)


def setup_inputs(seed: int = 0) -> dict:
    key_list = jax.random.split(jax.random.key(seed), 8)
    innovations = centred(key_list[0], (CH, TOTAL_OBS), 1.0, 6.0, ((1, 128),), jnp.float32)
    owner_tile_keys = jax.random.split(jax.random.fold_in(key_list[1], 1), TOTAL_OBS // OBS_DEV)
    owner_tile_turns = jax.random.permutation(jax.random.fold_in(key_list[1], 3), TOTAL_OBS // OBS_DEV)
    owner_tile = jax.vmap(lambda own, number: shared_out(jax.random.fold_in(key_list[1], 2), own, number, OBS_DEV, N_LON * N_LAT, 1, CAP, 2))(owner_tile_keys, owner_tile_turns).reshape((TOTAL_OBS, 1))
    obs_column = plant(jax.random.randint(key_list[2], (TOTAL_OBS,), 0, CY * CX), jax.random.fold_in(key_list[2], 1), 0, (CY * CX) - 1).astype(jnp.int32)
    obs_depth = plant(jax.random.randint(key_list[3], (TOTAL_OBS,), 1, LEVELS + 1), jax.random.fold_in(key_list[3], 1), 1, LEVELS).astype(jnp.int32)
    coefficients = jnp.clip(jnp.exp(math.log(0.25) - 2.1202636 * jax.random.uniform(key_list[4], (9, NY, NX), jnp.float32) ** shard_levels(key_list[4], (9, NY, NX), ((1, 8), (2, 16)), -0.2, 0.2)), 0.03, 0.25)
    sea_depth = plant(jax.random.randint(key_list[5], (NY, NX), 0, LEVELS + 1), jax.random.fold_in(key_list[5], 1), 0, LEVELS).astype(jnp.int32)
    balance = centred(key_list[6], (CH, CH), CH ** -0.5, 0.5, (), jnp.float32)
    return dict(innovations=innovations, owner_tile=owner_tile, obs_column=obs_column, obs_depth=obs_depth, coefficients=coefficients, sea_depth=sea_depth, balance=balance)


def extend_grid(array):
    lead = [(0, 0)] * (array.ndim - 2)
    array = jnp.pad(array, lead + [(1, 1), (0, 0)])
    return jnp.pad(array, lead + [(0, 0), (1, 1)], mode="wrap")


def reference(innovations, owner_tile, obs_column, obs_depth, coefficients, sea_depth, balance):
    level_ids = jnp.arange(CH) % LEVELS
    kept = jnp.where(level_ids[:, None] < obs_depth[None, :], innovations, 0.0)
    owners = owner_tile[:, 0]
    glob_y = (owners % N_LAT) * CY + obs_column // CX
    glob_x = (owners // N_LAT) * CX + obs_column % CX
    field = jnp.zeros((CH, NY, NX), jnp.float32).at[:, glob_y, glob_x].add(kept)
    coef_pad = extend_grid(coefficients)
    wet = (level_ids[:, None, None] < sea_depth[None, :, :]).astype(jnp.float32)

    def plane_pass(plane):
        padded = extend_grid(plane)
        summed = jnp.zeros((NY, NX), plane.dtype)
        for step_y in (-1, 0, 1):
            for step_x in (-1, 0, 1):
                offset = (step_y + 1) * 3 + step_x + 1
                row_start = 1 - step_y
                col_start = 1 - step_x
                summed = summed + coef_pad[offset, row_start:row_start + NY, col_start:col_start + NX] * padded[row_start:row_start + NY, col_start:col_start + NX]
        return summed

    for pass_index in range(PASSES):
        masked = lax.map(plane_pass, field) * wet
        field = jnp.einsum("cyx,cd->dyx", masked, balance, precision=lax.Precision.HIGHEST)
    return field
```

```python
import jax
import jax.numpy as jnp
from jax import lax
from jax.experimental import pallas as pl
from jax.experimental.pallas import tpu as pltpu
from jax.sharding import PartitionSpec as P

LEVELS = 75
PASSES = 4
RADIUS = PASSES
LANES = 256
CPAD = 152
CHUNK = 8


def shift_lon(block, step):
    count = lax.axis_size("lon")
    return lax.ppermute(block, "lon", [(i, (i + step) % count) for i in range(count)])


def shift_lat(block, step):
    count = lax.axis_size("lat")
    return lax.ppermute(
        block, "lat", [(i, i + step) for i in range(count) if 0 <= i + step < count]
    )


def shift_both(block, step_lon, step_lat):
    n_lon = lax.axis_size("lon")
    n_lat = lax.axis_size("lat")
    pairs = []
    for i in range(n_lon):
        for j in range(n_lat):
            if 0 <= j + step_lat < n_lat:
                pairs.append((i * n_lat + j, ((i + step_lon) % n_lon) * n_lat + j + step_lat))
    return lax.ppermute(block, ("lon", "lat"), pairs)


def with_halo(v):
    rows, ch, cols = v.shape
    r = RADIUS

    def dense(a):
        return a.reshape(a.shape[0], ch * r)

    def back(a, n):
        return a.reshape(n, ch, r)

    west = back(shift_lon(dense(v[:, :, cols - r :]), 1), rows)
    east = back(shift_lon(dense(v[:, :, :r]), -1), rows)
    south = shift_lat(v[rows - r :], 1)
    north = shift_lat(v[:r], -1)
    sw = back(shift_both(dense(v[rows - r :, :, cols - r :]), 1, 1), r)
    se = back(shift_both(dense(v[rows - r :, :, :r]), -1, 1), r)
    nw = back(shift_both(dense(v[:r, :, cols - r :]), 1, -1), r)
    ne = back(shift_both(dense(v[:r, :, :r]), -1, -1), r)
    top = jnp.concatenate([sw, south, se], axis=2)
    mid = jnp.concatenate([west, v, east], axis=2)
    bot = jnp.concatenate([nw, north, ne], axis=2)
    full = jnp.concatenate([top, mid, bot], axis=0)
    return jnp.pad(full, ((0, 0), (0, 0), (0, LANES - cols - 2 * r)))


def passes_kernel(p_ref, s_ref, lvl_ref, bal_ref, out_ref, a_ref, b_ref, u_ref):
    full = p_ref.shape[0]
    chans = p_ref.shape[1]
    out_ch = out_ref.shape[1]
    out_x = out_ref.shape[2]
    srcs = [p_ref, a_ref, b_ref, a_ref]
    dsts = [a_ref, b_ref, a_ref, None]
    for p in range(PASSES):
        src = srcs[p]
        dst = dsts[p]

        def row(y, carry, src=src, dst=dst):
            srows = [s_ref[y - dy] for dy in (-1, 0, 1)]
            coefs = {}
            for dy in (-1, 0, 1):
                for dx in (-1, 0, 1):
                    k = (dy + 1) * 3 + dx + 1
                    coefs[(dy, dx)] = jnp.broadcast_to(
                        srows[dy + 1][k : k + 1, :], (CHUNK, LANES)
                    )
            depth = jnp.broadcast_to(srows[1][9:10, :], (CHUNK, LANES))
            for c0 in range(0, chans, CHUNK):
                sums = [None, None, None]
                for dy in (-1, 0, 1):
                    v = src[y - dy, c0 : c0 + CHUNK, :]
                    for dx in (-1, 0, 1):
                        t = coefs[(dy, dx)] * v
                        sums[dx + 1] = t if sums[dx + 1] is None else sums[dx + 1] + t
                acc = (
                    sums[1]
                    + pltpu.roll(sums[0], LANES - 1, 1)
                    + pltpu.roll(sums[2], 1, 1)
                )
                u_ref[c0 : c0 + CHUNK, :] = jnp.where(
                    lvl_ref[c0 : c0 + CHUNK, :] < depth, acc, 0.0
                )
            res = jnp.dot(
                bal_ref[...],
                u_ref[...],
                precision=lax.Precision.HIGHEST,
                preferred_element_type=jnp.float32,
            )
            if dst is None:
                shifted = pltpu.roll(res, LANES - RADIUS, 1)
                out_ref[y - RADIUS] = shifted[:out_ch, :out_x]
            else:
                dst[y] = res
            return carry

        lax.fori_loop(p + 1, full - 1 - p, row, 0)


def run_passes(padded, stat, balance, rows, chans, cols):
    full = padded.shape[0]
    lvl = jnp.broadcast_to(
        (jnp.arange(CPAD) % LEVELS).astype(jnp.float32)[:, None], (CPAD, LANES)
    )
    bal_t = jnp.pad(balance.T, ((0, CPAD - chans), (0, CPAD - chans)))
    vmem = pltpu.VMEM
    work = full * CPAD * LANES
    return pl.pallas_call(
        passes_kernel,
        out_shape=jax.ShapeDtypeStruct((rows, chans, cols), jnp.float32),
        in_specs=[pl.BlockSpec(memory_space=vmem)] * 4,
        out_specs=pl.BlockSpec(memory_space=vmem),
        scratch_shapes=[
            vmem(padded.shape, jnp.float32),
            vmem(padded.shape, jnp.float32),
            vmem((CPAD, LANES), jnp.float32),
        ],
        compiler_params=pltpu.CompilerParams(vmem_limit_bytes=62 * 1024 * 1024),
        cost_estimate=pl.CostEstimate(
            flops=PASSES * (work * 20 + 2 * full * CPAD * CPAD * LANES),
            bytes_accessed=4 * (work + rows * chans * cols),
            transcendentals=0,
        ),
    )(padded, stat, lvl, bal_t)


def local(innovations, owner_tile, obs_column, obs_depth, coefficients, sea_depth, balance):
    channels = innovations.shape[0]
    obs_count = innovations.shape[1]
    devices = lax.axis_size("lon") * lax.axis_size("lat")
    capacity = 4 * obs_count // devices
    rows_y = sea_depth.shape[0]
    cols_x = sea_depth.shape[1]

    stat = jnp.concatenate([coefficients, sea_depth.astype(jnp.float32)[None]], axis=0)
    stat = with_halo(jnp.transpose(stat, (1, 0, 2)))

    level_ids = jnp.arange(channels) % LEVELS
    kept = jnp.where(level_ids[:, None] < obs_depth[None, :], innovations, 0.0)
    targets = owner_tile[:, 0]
    one_hot = (targets[:, None] == jnp.arange(devices, dtype=jnp.int32)[None, :]).astype(jnp.int32)
    before = jnp.cumsum(one_hot, axis=0) - one_hot
    slot_rank = jnp.sum(before * one_hot, axis=1)
    destination = targets * capacity + slot_rank
    payload = jnp.concatenate([kept.T, obs_column.astype(jnp.float32)[:, None]], axis=1)
    send = jnp.zeros((devices * capacity, channels + 1), jnp.float32).at[destination].set(payload)
    got = lax.all_to_all(
        send.reshape(devices, capacity, channels + 1), ("lon", "lat"), 0, 0, tiled=True
    ).reshape(devices * capacity, channels + 1)
    where = got[:, channels].astype(jnp.int32)
    field = jnp.zeros((rows_y * cols_x, channels), jnp.float32).at[where].add(got[:, :channels])
    field = jnp.transpose(field.reshape(rows_y, cols_x, channels), (0, 2, 1))
    field = jnp.pad(field, ((0, 0), (0, CPAD - channels), (0, 0)))
    padded = with_halo(field)
    out = run_passes(padded, stat, balance, rows_y, channels, cols_x)
    return jnp.transpose(out, (1, 0, 2))


def solution(mesh):
    placed = (
        P(None, ("lon", "lat")),
        P(("lon", "lat"), None),
        P(("lon", "lat")),
        P(("lon", "lat")),
        P(None, "lat", "lon"),
        P("lat", "lon"),
        P(),
    )
    return jax.shard_map(
        local, mesh=mesh, in_specs=placed, out_specs=P(None, "lat", "lon"), check_vma=False
    )
```

```python
import jax
import jax.numpy as jnp
from jax import lax
from jax.experimental import pallas as pl
from jax.experimental.pallas import tpu as pltpu
from jax.sharding import PartitionSpec as P

LEVELS = 75
PASSES = 4
RADIUS = PASSES
LANES = 256
CPAD = 152
CHUNK = 8


def shift_lon(block, step):
    count = lax.axis_size("lon")
    return lax.ppermute(block, "lon", [(i, (i + step) % count) for i in range(count)])


def shift_lat(block, step):
    count = lax.axis_size("lat")
    return lax.ppermute(
        block, "lat", [(i, i + step) for i in range(count) if 0 <= i + step < count]
    )


def shift_both(block, step_lon, step_lat):
    n_lon = lax.axis_size("lon")
    n_lat = lax.axis_size("lat")
    pairs = []
    for i in range(n_lon):
        for j in range(n_lat):
            if 0 <= j + step_lat < n_lat:
                pairs.append((i * n_lat + j, ((i + step_lon) % n_lon) * n_lat + j + step_lat))
    return lax.ppermute(block, ("lon", "lat"), pairs)


DIRECTIONS = (
    ("west", lambda v, r: v[:, :, v.shape[2] - r :], "lon", 1, 0),
    ("east", lambda v, r: v[:, :, :r], "lon", -1, 0),
    ("south", lambda v, r: v[v.shape[0] - r :], "lat", 0, 1),
    ("north", lambda v, r: v[:r], "lat", 0, -1),
    ("sw", lambda v, r: v[v.shape[0] - r :, :, v.shape[2] - r :], "both", 1, 1),
    ("se", lambda v, r: v[v.shape[0] - r :, :, :r], "both", -1, 1),
    ("nw", lambda v, r: v[:r, :, v.shape[2] - r :], "both", 1, -1),
    ("ne", lambda v, r: v[:r, :, :r], "both", -1, -1),
)


def exchange(parts):
    got = [dict() for _ in parts]
    for name, take, axis, step_lon, step_lat in DIRECTIONS:
        pieces = [take(v, RADIUS) for v in parts]
        flat = jnp.concatenate([p.reshape(-1) for p in pieces])
        if axis == "lon":
            flat = shift_lon(flat, step_lon)
        elif axis == "lat":
            flat = shift_lat(flat, step_lat)
        else:
            flat = shift_both(flat, step_lon, step_lat)
        offset = 0
        for i, p in enumerate(pieces):
            got[i][name] = flat[offset : offset + p.size].reshape(p.shape)
            offset += p.size
    return got


def side_lanes(east, west, gap):
    zeros = jnp.zeros(east.shape[:2] + (gap,), jnp.float32)
    return jnp.concatenate([east, zeros, west], axis=2)


def assemble(v, h):
    cols = v.shape[2]
    gap = LANES - cols - 2 * RADIUS
    top = jnp.concatenate([h["south"], side_lanes(h["se"], h["sw"], gap)], axis=2)
    mid = jnp.concatenate([v, side_lanes(h["east"], h["west"], gap)], axis=2)
    bot = jnp.concatenate([h["north"], side_lanes(h["ne"], h["nw"], gap)], axis=2)
    return jnp.concatenate([top, mid, bot], axis=0)


def split_bf16(x):
    hi = x.astype(jnp.bfloat16)
    lo = (x - hi.astype(jnp.float32)).astype(jnp.bfloat16)
    return hi, lo


def passes_kernel(
    v_ref, ew_ref, top_ref, bot_ref, s_ref, lvl_ref, bal_ref, out_ref, a_ref, b_ref, p_ref, u_ref
):
    full = p_ref.shape[0]
    rows = v_ref.shape[0]
    cols = v_ref.shape[2]
    chans = p_ref.shape[1]
    out_ch = out_ref.shape[1]
    p_ref[:RADIUS] = top_ref[...]
    p_ref[full - RADIUS :] = bot_ref[...]

    def fill(y, carry):
        p_ref[y + RADIUS, :, :cols] = v_ref[y]
        p_ref[y + RADIUS, :, cols:] = ew_ref[y]
        return carry

    lax.fori_loop(0, rows, fill, 0)
    b_hi, b_lo = split_bf16(bal_ref[...])
    srcs = [p_ref, a_ref, b_ref, a_ref]
    dsts = [a_ref, b_ref, a_ref, None]
    for p in range(PASSES):
        src = srcs[p]
        dst = dsts[p]

        def row(y, carry, src=src, dst=dst):
            srows = [s_ref[y - dy] for dy in (-1, 0, 1)]
            coefs = {}
            for dy in (-1, 0, 1):
                for dx in (-1, 0, 1):
                    k = (dy + 1) * 3 + dx + 1
                    coefs[(dy, dx)] = jnp.broadcast_to(
                        srows[dy + 1][k : k + 1, :], (CHUNK, LANES)
                    )
            depth = jnp.broadcast_to(srows[1][9:10, :], (CHUNK, LANES))
            for c0 in range(0, chans, CHUNK):
                sums = [None, None, None]
                for dy in (-1, 0, 1):
                    v = src[y - dy, c0 : c0 + CHUNK, :]
                    for dx in (-1, 0, 1):
                        t = coefs[(dy, dx)] * v
                        sums[dx + 1] = t if sums[dx + 1] is None else sums[dx + 1] + t
                acc = (
                    sums[1]
                    + pltpu.roll(sums[0], LANES - 1, 1)
                    + pltpu.roll(sums[2], 1, 1)
                )
                u_ref[c0 : c0 + CHUNK, :] = jnp.where(
                    lvl_ref[c0 : c0 + CHUNK, :] < depth, acc, 0.0
                )
            u_hi, u_lo = split_bf16(u_ref[...])
            res = jnp.dot(b_hi, u_hi, preferred_element_type=jnp.float32)
            res = res + jnp.dot(b_hi, u_lo, preferred_element_type=jnp.float32)
            res = res + jnp.dot(b_lo, u_hi, preferred_element_type=jnp.float32)
            if dst is None:
                out_ref[y - RADIUS] = res[:out_ch, :cols]
            else:
                dst[y] = res
            return carry

        lax.fori_loop(p + 1, full - 1 - p, row, 0, unroll=2)


def run_passes(field, halos, stat, balance, chans):
    rows, cpad, cols = field.shape
    full = rows + 2 * RADIUS
    gap = LANES - cols - 2 * RADIUS
    ew = side_lanes(halos["east"], halos["west"], gap)
    top = jnp.concatenate([halos["south"], side_lanes(halos["se"], halos["sw"], gap)], axis=2)
    bot = jnp.concatenate([halos["north"], side_lanes(halos["ne"], halos["nw"], gap)], axis=2)
    lvl = jnp.broadcast_to(
        (jnp.arange(CPAD) % LEVELS).astype(jnp.float32)[:, None], (CPAD, LANES)
    )
    bal_t = jnp.pad(balance.T, ((0, CPAD - chans), (0, CPAD - chans)))
    vmem = pltpu.VMEM
    work = full * CPAD * LANES
    return pl.pallas_call(
        passes_kernel,
        out_shape=jax.ShapeDtypeStruct((rows, chans, cols), jnp.float32),
        in_specs=[pl.BlockSpec(memory_space=vmem)] * 7,
        out_specs=pl.BlockSpec(memory_space=vmem),
        scratch_shapes=[
            vmem((full, CPAD, LANES), jnp.float32),
            vmem((full, CPAD, LANES), jnp.float32),
            vmem((full, CPAD, LANES), jnp.float32),
            vmem((CPAD, LANES), jnp.float32),
        ],
        compiler_params=pltpu.CompilerParams(vmem_limit_bytes=62 * 1024 * 1024),
        cost_estimate=pl.CostEstimate(
            flops=PASSES * (work * 20 + 6 * full * CPAD * CPAD * LANES),
            bytes_accessed=4 * (work + rows * chans * cols),
            transcendentals=0,
        ),
    )(field, ew, top, bot, stat, lvl, bal_t)


def local(innovations, owner_tile, obs_column, obs_depth, coefficients, sea_depth, balance):
    channels = innovations.shape[0]
    obs_count = innovations.shape[1]
    devices = lax.axis_size("lon") * lax.axis_size("lat")
    capacity = 4 * obs_count // devices
    rows_y = sea_depth.shape[0]
    cols_x = sea_depth.shape[1]

    stat = jnp.concatenate([coefficients, sea_depth.astype(jnp.float32)[None]], axis=0)
    stat = jnp.transpose(stat, (1, 0, 2))

    level_ids = jnp.arange(channels) % LEVELS
    kept = jnp.where(level_ids[:, None] < obs_depth[None, :], innovations, 0.0)
    targets = owner_tile[:, 0]
    one_hot = (targets[:, None] == jnp.arange(devices, dtype=jnp.int32)[None, :]).astype(jnp.int32)
    before = jnp.cumsum(one_hot, axis=0) - one_hot
    slot_rank = jnp.sum(before * one_hot, axis=1)
    destination = targets * capacity + slot_rank
    payload = jnp.concatenate([kept.T, obs_column.astype(jnp.float32)[:, None]], axis=1)
    send = jnp.zeros((devices * capacity, channels + 1), jnp.float32).at[destination].set(payload)
    got = lax.all_to_all(
        send.reshape(devices, capacity, channels + 1), ("lon", "lat"), 0, 0, tiled=True
    ).reshape(devices * capacity, channels + 1)
    where = got[:, channels].astype(jnp.int32)
    field = jnp.zeros((rows_y * cols_x, channels), jnp.float32).at[where].add(got[:, :channels])
    field = jnp.transpose(field.reshape(rows_y, cols_x, channels), (0, 2, 1))
    field = jnp.pad(field, ((0, 0), (0, CPAD - channels), (0, 0)))
    field_halo, stat_halo = exchange([field, stat])
    stat = assemble(stat, stat_halo)
    out = run_passes(field, field_halo, stat, balance, channels)
    return jnp.transpose(out, (1, 0, 2))


def solution(mesh):
    placed = (
        P(None, ("lon", "lat")),
        P(("lon", "lat"), None),
        P(("lon", "lat")),
        P(("lon", "lat")),
        P(None, "lat", "lon"),
        P("lat", "lon"),
        P(),
    )
    return jax.shard_map(
        local, mesh=mesh, in_specs=placed, out_specs=P(None, "lat", "lon"), check_vma=False
    )
```

```python
import jax
import jax.numpy as jnp
from jax import lax
from jax.experimental import pallas as pl
from jax.experimental.pallas import tpu as pltpu
from jax.sharding import PartitionSpec as P

LEVELS = 75
PASSES = 4
RADIUS = PASSES
LANES = 256
CPAD = 152
CHUNK = 8


def shift_lon(block, step):
    count = lax.axis_size("lon")
    return lax.ppermute(block, "lon", [(i, (i + step) % count) for i in range(count)])


def shift_lat(block, step):
    count = lax.axis_size("lat")
    return lax.ppermute(
        block, "lat", [(i, i + step) for i in range(count) if 0 <= i + step < count]
    )


def shift_both(block, step_lon, step_lat):
    n_lon = lax.axis_size("lon")
    n_lat = lax.axis_size("lat")
    pairs = []
    for i in range(n_lon):
        for j in range(n_lat):
            if 0 <= j + step_lat < n_lat:
                pairs.append((i * n_lat + j, ((i + step_lon) % n_lon) * n_lat + j + step_lat))
    return lax.ppermute(block, ("lon", "lat"), pairs)


DIRECTIONS = (
    ("west", lambda v, r: v[:, :, v.shape[2] - r :], "lon", 1, 0),
    ("east", lambda v, r: v[:, :, :r], "lon", -1, 0),
    ("south", lambda v, r: v[v.shape[0] - r :], "lat", 0, 1),
    ("north", lambda v, r: v[:r], "lat", 0, -1),
    ("sw", lambda v, r: v[v.shape[0] - r :, :, v.shape[2] - r :], "both", 1, 1),
    ("se", lambda v, r: v[v.shape[0] - r :, :, :r], "both", -1, 1),
    ("nw", lambda v, r: v[:r, :, v.shape[2] - r :], "both", 1, -1),
    ("ne", lambda v, r: v[:r, :, :r], "both", -1, -1),
)


def exchange(parts):
    got = [dict() for _ in parts]
    for name, take, axis, step_lon, step_lat in DIRECTIONS:
        pieces = [take(v, RADIUS) for v in parts]
        flat = jnp.concatenate([p.reshape(-1) for p in pieces])
        if axis == "lon":
            flat = shift_lon(flat, step_lon)
        elif axis == "lat":
            flat = shift_lat(flat, step_lat)
        else:
            flat = shift_both(flat, step_lon, step_lat)
        offset = 0
        for i, p in enumerate(pieces):
            got[i][name] = flat[offset : offset + p.size].reshape(p.shape)
            offset += p.size
    return got


def field_halos(f):
    rows, cols, _ = f.shape
    r = RADIUS
    v_top = jnp.transpose(f[:r], (0, 2, 1))
    v_bot = jnp.transpose(f[rows - r :], (0, 2, 1))

    def t(a):
        return jnp.transpose(a, (0, 2, 1))

    return {
        "west": t(shift_lon(f[:, cols - r :, :], 1)),
        "east": t(shift_lon(f[:, :r, :], -1)),
        "south": shift_lat(v_bot, 1),
        "north": shift_lat(v_top, -1),
        "sw": t(shift_both(f[rows - r :, cols - r :, :], 1, 1)),
        "se": t(shift_both(f[rows - r :, :r, :], -1, 1)),
        "nw": t(shift_both(f[:r, cols - r :, :], 1, -1)),
        "ne": t(shift_both(f[:r, :r, :], -1, -1)),
    }


def side_lanes(east, west, gap):
    zeros = jnp.zeros(east.shape[:2] + (gap,), jnp.float32)
    return jnp.concatenate([east, zeros, west], axis=2)


def assemble(v, h):
    cols = v.shape[2]
    gap = LANES - cols - 2 * RADIUS
    top = jnp.concatenate([h["south"], side_lanes(h["se"], h["sw"], gap)], axis=2)
    mid = jnp.concatenate([v, side_lanes(h["east"], h["west"], gap)], axis=2)
    bot = jnp.concatenate([h["north"], side_lanes(h["ne"], h["nw"], gap)], axis=2)
    return jnp.concatenate([top, mid, bot], axis=0)


def split_bf16(x):
    hi = x.astype(jnp.bfloat16)
    lo = (x - hi.astype(jnp.float32)).astype(jnp.bfloat16)
    return hi, lo


def passes_kernel(
    v_ref, ew_ref, top_ref, bot_ref, s_ref, lvl_ref, bal_ref, out_ref, a_ref, b_ref, p_ref, u_ref
):
    full = p_ref.shape[0]
    rows = v_ref.shape[0]
    cols = v_ref.shape[2]
    chans = p_ref.shape[1]
    out_ch = out_ref.shape[1]
    p_ref[:RADIUS] = top_ref[...]
    p_ref[full - RADIUS :] = bot_ref[...]

    def fill(y, carry):
        p_ref[y + RADIUS, :, :cols] = v_ref[y]
        p_ref[y + RADIUS, :, cols:] = ew_ref[y]
        return carry

    lax.fori_loop(0, rows, fill, 0)
    b_hi, b_lo = split_bf16(bal_ref[...])
    srcs = [p_ref, a_ref, b_ref, a_ref]
    dsts = [a_ref, b_ref, a_ref, None]
    for p in range(PASSES):
        src = srcs[p]
        dst = dsts[p]

        def row(y, carry, src=src, dst=dst):
            srows = [s_ref[y - dy] for dy in (-1, 0, 1)]
            coefs = {}
            for dy in (-1, 0, 1):
                for dx in (-1, 0, 1):
                    k = (dy + 1) * 3 + dx + 1
                    coefs[(dy, dx)] = jnp.broadcast_to(
                        srows[dy + 1][k : k + 1, :], (CHUNK, LANES)
                    )
            depth = jnp.broadcast_to(srows[1][9:10, :], (CHUNK, LANES))
            for c0 in range(0, chans, CHUNK):
                sums = [None, None, None]
                for dy in (-1, 0, 1):
                    v = src[y - dy, c0 : c0 + CHUNK, :]
                    for dx in (-1, 0, 1):
                        t = coefs[(dy, dx)] * v
                        sums[dx + 1] = t if sums[dx + 1] is None else sums[dx + 1] + t
                acc = (
                    sums[1]
                    + pltpu.roll(sums[0], LANES - 1, 1)
                    + pltpu.roll(sums[2], 1, 1)
                )
                u_ref[c0 : c0 + CHUNK, :] = jnp.where(
                    lvl_ref[c0 : c0 + CHUNK, :] < depth, acc, 0.0
                )
            u_hi, u_lo = split_bf16(u_ref[...])
            res = jnp.dot(b_hi, u_hi, preferred_element_type=jnp.float32)
            res = res + jnp.dot(b_hi, u_lo, preferred_element_type=jnp.float32)
            res = res + jnp.dot(b_lo, u_hi, preferred_element_type=jnp.float32)
            if dst is None:
                out_ref[y - RADIUS] = res[:out_ch, :cols]
            else:
                dst[y] = res
            return carry

        lax.fori_loop(p + 1, full - 1 - p, row, 0, unroll=2)


def run_passes(field_pm, halos, stat, balance, chans):
    field = jnp.transpose(field_pm, (0, 2, 1))
    rows, cpad, cols = field.shape
    full = rows + 2 * RADIUS
    gap = LANES - cols - 2 * RADIUS
    ew = side_lanes(halos["east"], halos["west"], gap)
    top = jnp.concatenate([halos["south"], side_lanes(halos["se"], halos["sw"], gap)], axis=2)
    bot = jnp.concatenate([halos["north"], side_lanes(halos["ne"], halos["nw"], gap)], axis=2)
    lvl = jnp.broadcast_to(
        (jnp.arange(CPAD) % LEVELS).astype(jnp.float32)[:, None], (CPAD, LANES)
    )
    bal_t = jnp.pad(balance.T, ((0, CPAD - chans), (0, CPAD - chans)))
    vmem = pltpu.VMEM
    work = full * CPAD * LANES
    return pl.pallas_call(
        passes_kernel,
        out_shape=jax.ShapeDtypeStruct((rows, chans, cols), jnp.float32),
        in_specs=[pl.BlockSpec(memory_space=vmem)] * 7,
        out_specs=pl.BlockSpec(memory_space=vmem),
        scratch_shapes=[
            vmem((full, CPAD, LANES), jnp.float32),
            vmem((full, CPAD, LANES), jnp.float32),
            vmem((full, CPAD, LANES), jnp.float32),
            vmem((CPAD, LANES), jnp.float32),
        ],
        compiler_params=pltpu.CompilerParams(vmem_limit_bytes=62 * 1024 * 1024),
        cost_estimate=pl.CostEstimate(
            flops=PASSES * (work * 20 + 6 * full * CPAD * CPAD * LANES),
            bytes_accessed=4 * (work + rows * chans * cols),
            transcendentals=0,
        ),
    )(field, ew, top, bot, stat, lvl, bal_t)


def local(innovations, owner_tile, obs_column, obs_depth, coefficients, sea_depth, balance):
    channels = innovations.shape[0]
    obs_count = innovations.shape[1]
    devices = lax.axis_size("lon") * lax.axis_size("lat")
    capacity = 4 * obs_count // devices
    rows_y = sea_depth.shape[0]
    cols_x = sea_depth.shape[1]

    stat = jnp.concatenate([coefficients, sea_depth.astype(jnp.float32)[None]], axis=0)
    stat = jnp.transpose(stat, (1, 0, 2))

    level_ids = jnp.arange(channels) % LEVELS
    kept = jnp.where(level_ids[:, None] < obs_depth[None, :], innovations, 0.0)
    targets = owner_tile[:, 0]
    one_hot = (targets[:, None] == jnp.arange(devices, dtype=jnp.int32)[None, :]).astype(jnp.int32)
    before = jnp.cumsum(one_hot, axis=0) - one_hot
    slot_rank = jnp.sum(before * one_hot, axis=1)
    destination = targets * capacity + slot_rank
    payload = jnp.concatenate(
        [
            kept.T,
            jnp.zeros((obs_count, CPAD - channels - 1), jnp.float32),
            obs_column.astype(jnp.float32)[:, None],
        ],
        axis=1,
    )
    send = jnp.zeros((devices * capacity, CPAD), jnp.float32).at[destination].set(payload)
    got = lax.all_to_all(
        send.reshape(devices, capacity, CPAD), ("lon", "lat"), 0, 0, tiled=True
    ).reshape(devices * capacity, CPAD)
    where = got[:, CPAD - 1].astype(jnp.int32)
    field = jnp.zeros((rows_y * cols_x, CPAD), jnp.float32).at[where].add(got)
    field = field.reshape(rows_y, cols_x, CPAD)
    (stat_halo,) = exchange([stat])
    stat = assemble(stat, stat_halo)
    out = run_passes(field, field_halos(field), stat, balance, channels)
    return jnp.transpose(out, (1, 0, 2))


def solution(mesh):
    placed = (
        P(None, ("lon", "lat")),
        P(("lon", "lat"), None),
        P(("lon", "lat")),
        P(("lon", "lat")),
        P(None, "lat", "lon"),
        P("lat", "lon"),
        P(),
    )
    return jax.shard_map(
        local, mesh=mesh, in_specs=placed, out_specs=P(None, "lat", "lon"), check_vma=False
    )
```

```python
import jax
import jax.numpy as jnp
from jax import lax
from jax.experimental import pallas as pl
from jax.experimental.pallas import tpu as pltpu
from jax.sharding import PartitionSpec as P

LEVELS = 75
PASSES = 4
RADIUS = PASSES
LANES = 256
CPAD = 152
CHUNK = 8


def shift_lon(block, step):
    count = lax.axis_size("lon")
    return lax.ppermute(block, "lon", [(i, (i + step) % count) for i in range(count)])


def shift_lat(block, step):
    count = lax.axis_size("lat")
    return lax.ppermute(
        block, "lat", [(i, i + step) for i in range(count) if 0 <= i + step < count]
    )


def shift_both(block, step_lon, step_lat):
    n_lon = lax.axis_size("lon")
    n_lat = lax.axis_size("lat")
    pairs = []
    for i in range(n_lon):
        for j in range(n_lat):
            if 0 <= j + step_lat < n_lat:
                pairs.append((i * n_lat + j, ((i + step_lon) % n_lon) * n_lat + j + step_lat))
    return lax.ppermute(block, ("lon", "lat"), pairs)


DIRECTIONS = (
    ("west", lambda v, r: v[:, :, v.shape[2] - r :], "lon", 1, 0),
    ("east", lambda v, r: v[:, :, :r], "lon", -1, 0),
    ("south", lambda v, r: v[v.shape[0] - r :], "lat", 0, 1),
    ("north", lambda v, r: v[:r], "lat", 0, -1),
    ("sw", lambda v, r: v[v.shape[0] - r :, :, v.shape[2] - r :], "both", 1, 1),
    ("se", lambda v, r: v[v.shape[0] - r :, :, :r], "both", -1, 1),
    ("nw", lambda v, r: v[:r, :, v.shape[2] - r :], "both", 1, -1),
    ("ne", lambda v, r: v[:r, :, :r], "both", -1, -1),
)


def exchange(parts):
    got = [dict() for _ in parts]
    for name, take, axis, step_lon, step_lat in DIRECTIONS:
        pieces = [take(v, RADIUS) for v in parts]
        flat = jnp.concatenate([p.reshape(-1) for p in pieces])
        if axis == "lon":
            flat = shift_lon(flat, step_lon)
        elif axis == "lat":
            flat = shift_lat(flat, step_lat)
        else:
            flat = shift_both(flat, step_lon, step_lat)
        offset = 0
        for i, p in enumerate(pieces):
            got[i][name] = flat[offset : offset + p.size].reshape(p.shape)
            offset += p.size
    return got


def field_halos(f):
    rows, cols, _ = f.shape
    r = RADIUS
    v_top = jnp.transpose(f[:r], (0, 2, 1))
    v_bot = jnp.transpose(f[rows - r :], (0, 2, 1))

    def t(a):
        return jnp.transpose(a, (0, 2, 1))

    return {
        "west": shift_lon(f[:, cols - r :, :], 1),
        "east": shift_lon(f[:, :r, :], -1),
        "south": shift_lat(v_bot, 1),
        "north": shift_lat(v_top, -1),
        "sw": t(shift_both(f[rows - r :, cols - r :, :], 1, 1)),
        "se": t(shift_both(f[rows - r :, :r, :], -1, 1)),
        "nw": t(shift_both(f[:r, cols - r :, :], 1, -1)),
        "ne": t(shift_both(f[:r, :r, :], -1, -1)),
    }


def side_lanes(east, west, gap):
    zeros = jnp.zeros(east.shape[:2] + (gap,), jnp.float32)
    return jnp.concatenate([east, zeros, west], axis=2)


def assemble(v, h):
    cols = v.shape[2]
    gap = LANES - cols - 2 * RADIUS
    top = jnp.concatenate([h["south"], side_lanes(h["se"], h["sw"], gap)], axis=2)
    mid = jnp.concatenate([v, side_lanes(h["east"], h["west"], gap)], axis=2)
    bot = jnp.concatenate([h["north"], side_lanes(h["ne"], h["nw"], gap)], axis=2)
    return jnp.concatenate([top, mid, bot], axis=0)


def split_bf16(x):
    hi = x.astype(jnp.bfloat16)
    lo = (x - hi.astype(jnp.float32)).astype(jnp.bfloat16)
    return hi, lo


def passes_kernel(
    v_ref, ew_ref, top_ref, bot_ref, s_ref, lvl_ref, bal_ref, out_ref, a_ref, b_ref, p_ref, u_ref
):
    full = p_ref.shape[0]
    rows = v_ref.shape[0]
    cols = v_ref.shape[1]
    chans = p_ref.shape[1]
    out_ch = out_ref.shape[1]
    p_ref[:RADIUS] = top_ref[...]
    p_ref[full - RADIUS :] = bot_ref[...]

    def fill(y, carry):
        p_ref[y + RADIUS, :, :cols] = jnp.transpose(v_ref[y])
        p_ref[y + RADIUS, :, cols:] = jnp.zeros((chans, LANES - cols), jnp.float32)
        sides = jnp.transpose(ew_ref[y])
        p_ref[y + RADIUS, :, cols : cols + RADIUS] = sides[:, :RADIUS]
        p_ref[y + RADIUS, :, LANES - RADIUS :] = sides[:, RADIUS:]
        return carry

    lax.fori_loop(0, rows, fill, 0)
    b_hi, b_lo = split_bf16(bal_ref[...])
    srcs = [p_ref, a_ref, b_ref, a_ref]
    dsts = [a_ref, b_ref, a_ref, None]
    for p in range(PASSES):
        src = srcs[p]
        dst = dsts[p]

        def row(y, carry, src=src, dst=dst):
            srows = [s_ref[y - dy] for dy in (-1, 0, 1)]
            coefs = {}
            for dy in (-1, 0, 1):
                for dx in (-1, 0, 1):
                    k = (dy + 1) * 3 + dx + 1
                    coefs[(dy, dx)] = jnp.broadcast_to(
                        srows[dy + 1][k : k + 1, :], (CHUNK, LANES)
                    )
            depth = jnp.broadcast_to(srows[1][9:10, :], (CHUNK, LANES))
            for c0 in range(0, chans, CHUNK):
                sums = [None, None, None]
                for dy in (-1, 0, 1):
                    v = src[y - dy, c0 : c0 + CHUNK, :]
                    for dx in (-1, 0, 1):
                        t = coefs[(dy, dx)] * v
                        sums[dx + 1] = t if sums[dx + 1] is None else sums[dx + 1] + t
                acc = (
                    sums[1]
                    + pltpu.roll(sums[0], LANES - 1, 1)
                    + pltpu.roll(sums[2], 1, 1)
                )
                u_ref[c0 : c0 + CHUNK, :] = jnp.where(
                    lvl_ref[c0 : c0 + CHUNK, :] < depth, acc, 0.0
                )
            u_hi, u_lo = split_bf16(u_ref[...])
            res = jnp.dot(b_hi, u_hi, preferred_element_type=jnp.float32)
            res = res + jnp.dot(b_hi, u_lo, preferred_element_type=jnp.float32)
            res = res + jnp.dot(b_lo, u_hi, preferred_element_type=jnp.float32)
            if dst is None:
                out_ref[y - RADIUS] = res[:out_ch, :cols]
            else:
                dst[y] = res
            return carry

        lax.fori_loop(p + 1, full - 1 - p, row, 0, unroll=2)


def run_passes(field, halos, stat, balance, chans):
    rows, cols, cpad = field.shape
    full = rows + 2 * RADIUS
    gap = LANES - cols - 2 * RADIUS
    ew = jnp.concatenate([halos["east"], halos["west"]], axis=1)
    top = jnp.concatenate([halos["south"], side_lanes(halos["se"], halos["sw"], gap)], axis=2)
    bot = jnp.concatenate([halos["north"], side_lanes(halos["ne"], halos["nw"], gap)], axis=2)
    lvl = jnp.broadcast_to(
        (jnp.arange(CPAD) % LEVELS).astype(jnp.float32)[:, None], (CPAD, LANES)
    )
    bal_t = jnp.pad(balance.T, ((0, CPAD - chans), (0, CPAD - chans)))
    vmem = pltpu.VMEM
    work = full * CPAD * LANES
    return pl.pallas_call(
        passes_kernel,
        out_shape=jax.ShapeDtypeStruct((rows, chans, cols), jnp.float32),
        in_specs=[pl.BlockSpec(memory_space=vmem)] * 7,
        out_specs=pl.BlockSpec(memory_space=vmem),
        scratch_shapes=[
            vmem((full, CPAD, LANES), jnp.float32),
            vmem((full, CPAD, LANES), jnp.float32),
            vmem((full, CPAD, LANES), jnp.float32),
            vmem((CPAD, LANES), jnp.float32),
        ],
        compiler_params=pltpu.CompilerParams(vmem_limit_bytes=62 * 1024 * 1024),
        cost_estimate=pl.CostEstimate(
            flops=PASSES * (work * 20 + 6 * full * CPAD * CPAD * LANES),
            bytes_accessed=4 * (work + rows * chans * cols),
            transcendentals=0,
        ),
    )(field, ew, top, bot, stat, lvl, bal_t)


def local(innovations, owner_tile, obs_column, obs_depth, coefficients, sea_depth, balance):
    channels = innovations.shape[0]
    obs_count = innovations.shape[1]
    devices = lax.axis_size("lon") * lax.axis_size("lat")
    capacity = 4 * obs_count // devices
    rows_y = sea_depth.shape[0]
    cols_x = sea_depth.shape[1]

    stat = jnp.concatenate([coefficients, sea_depth.astype(jnp.float32)[None]], axis=0)
    stat = jnp.transpose(stat, (1, 0, 2))

    level_ids = jnp.arange(channels) % LEVELS
    kept = jnp.where(level_ids[:, None] < obs_depth[None, :], innovations, 0.0)
    targets = owner_tile[:, 0]
    one_hot = (targets[:, None] == jnp.arange(devices, dtype=jnp.int32)[None, :]).astype(jnp.int32)
    before = jnp.cumsum(one_hot, axis=0) - one_hot
    slot_rank = jnp.sum(before * one_hot, axis=1)
    destination = targets * capacity + slot_rank
    payload = jnp.concatenate(
        [
            kept.T,
            jnp.zeros((obs_count, CPAD - channels - 1), jnp.float32),
            obs_column.astype(jnp.float32)[:, None],
        ],
        axis=1,
    )
    send = jnp.zeros((devices * capacity, CPAD), jnp.float32).at[destination].set(payload)
    got = lax.all_to_all(
        send.reshape(devices, capacity, CPAD), ("lon", "lat"), 0, 0, tiled=True
    ).reshape(devices * capacity, CPAD)
    where = got[:, CPAD - 1].astype(jnp.int32)
    field = jnp.zeros((rows_y * cols_x, CPAD), jnp.float32).at[where].add(got)
    field = field.reshape(rows_y, cols_x, CPAD)
    (stat_halo,) = exchange([stat])
    stat = assemble(stat, stat_halo)
    out = run_passes(field, field_halos(field), stat, balance, channels)
    return jnp.transpose(out, (1, 0, 2))


def solution(mesh):
    placed = (
        P(None, ("lon", "lat")),
        P(("lon", "lat"), None),
        P(("lon", "lat")),
        P(("lon", "lat")),
        P(None, "lat", "lon"),
        P("lat", "lon"),
        P(),
    )
    return jax.shard_map(
        local, mesh=mesh, in_specs=placed, out_specs=P(None, "lat", "lon"), check_vma=False
    )
```

```python
import jax
import jax.numpy as jnp
from jax import lax
from jax.experimental import pallas as pl
from jax.experimental.pallas import tpu as pltpu
from jax.sharding import PartitionSpec as P

LEVELS = 75
PASSES = 4
RADIUS = PASSES
LANES = 256
CPAD = 152
CHUNK = 8
SPAD = 16


def shift_lon(block, step):
    count = lax.axis_size("lon")
    return lax.ppermute(block, "lon", [(i, (i + step) % count) for i in range(count)])


def shift_lat(block, step):
    count = lax.axis_size("lat")
    return lax.ppermute(
        block, "lat", [(i, i + step) for i in range(count) if 0 <= i + step < count]
    )


def shift_both(block, step_lon, step_lat):
    n_lon = lax.axis_size("lon")
    n_lat = lax.axis_size("lat")
    pairs = []
    for i in range(n_lon):
        for j in range(n_lat):
            if 0 <= j + step_lat < n_lat:
                pairs.append((i * n_lat + j, ((i + step_lon) % n_lon) * n_lat + j + step_lat))
    return lax.ppermute(block, ("lon", "lat"), pairs)


DIRECTIONS = (
    ("west", lambda v, r: v[:, :, v.shape[2] - r :], "lon", 1, 0),
    ("east", lambda v, r: v[:, :, :r], "lon", -1, 0),
    ("south", lambda v, r: v[v.shape[0] - r :], "lat", 0, 1),
    ("north", lambda v, r: v[:r], "lat", 0, -1),
    ("sw", lambda v, r: v[v.shape[0] - r :, :, v.shape[2] - r :], "both", 1, 1),
    ("se", lambda v, r: v[v.shape[0] - r :, :, :r], "both", -1, 1),
    ("nw", lambda v, r: v[:r, :, v.shape[2] - r :], "both", 1, -1),
    ("ne", lambda v, r: v[:r, :, :r], "both", -1, -1),
)


def exchange(parts):
    got = [dict() for _ in parts]
    for name, take, axis, step_lon, step_lat in DIRECTIONS:
        pieces = [take(v, RADIUS) for v in parts]
        flat = jnp.concatenate([p.reshape(-1) for p in pieces])
        if axis == "lon":
            flat = shift_lon(flat, step_lon)
        elif axis == "lat":
            flat = shift_lat(flat, step_lat)
        else:
            flat = shift_both(flat, step_lon, step_lat)
        offset = 0
        for i, p in enumerate(pieces):
            got[i][name] = flat[offset : offset + p.size].reshape(p.shape)
            offset += p.size
    return got


def field_halos(f):
    rows, cols, _ = f.shape
    r = RADIUS
    v_top = jnp.transpose(f[:r], (0, 2, 1))
    v_bot = jnp.transpose(f[rows - r :], (0, 2, 1))

    def t(a):
        return jnp.transpose(a, (0, 2, 1))

    return {
        "west": shift_lon(f[:, cols - r :, :], 1),
        "east": shift_lon(f[:, :r, :], -1),
        "south": shift_lat(v_bot, 1),
        "north": shift_lat(v_top, -1),
        "sw": t(shift_both(f[rows - r :, cols - r :, :], 1, 1)),
        "se": t(shift_both(f[rows - r :, :r, :], -1, 1)),
        "nw": t(shift_both(f[:r, cols - r :, :], 1, -1)),
        "ne": t(shift_both(f[:r, :r, :], -1, -1)),
    }


def side_lanes(east, west, gap):
    zeros = jnp.zeros(east.shape[:2] + (gap,), jnp.float32)
    return jnp.concatenate([east, zeros, west], axis=2)


def assemble(v, h):
    cols = v.shape[2]
    gap = LANES - cols - 2 * RADIUS
    top = jnp.concatenate([h["south"], side_lanes(h["se"], h["sw"], gap)], axis=2)
    mid = jnp.concatenate([v, side_lanes(h["east"], h["west"], gap)], axis=2)
    bot = jnp.concatenate([h["north"], side_lanes(h["ne"], h["nw"], gap)], axis=2)
    return jnp.concatenate([top, mid, bot], axis=0)


def split_bf16(x):
    hi = x.astype(jnp.bfloat16)
    lo = (x - hi.astype(jnp.float32)).astype(jnp.bfloat16)
    return hi, lo


def passes_kernel(
    v_ref, ew_ref, top_ref, bot_ref, lvl_ref, bal_ref, out_ref, a_ref, b_ref, p_ref, s_ref, u_ref
):
    full = p_ref.shape[0]
    rows = v_ref.shape[0]
    cols = v_ref.shape[1]
    chans = p_ref.shape[1]
    out_ch = out_ref.shape[1]
    statc = s_ref.shape[1]
    p_ref[:RADIUS] = top_ref[:, :chans, :]
    s_ref[:RADIUS] = top_ref[:, chans:, :]
    p_ref[full - RADIUS :] = bot_ref[:, :chans, :]
    s_ref[full - RADIUS :] = bot_ref[:, chans:, :]

    def fill(y, carry):
        body = jnp.transpose(v_ref[y])
        sides = jnp.transpose(ew_ref[y])
        for ref, lo, n in ((p_ref, 0, chans), (s_ref, chans, statc)):
            ref[y + RADIUS, :, :cols] = body[lo : lo + n]
            ref[y + RADIUS, :, cols:] = jnp.zeros((n, LANES - cols), jnp.float32)
            ref[y + RADIUS, :, cols : cols + RADIUS] = sides[lo : lo + n, :RADIUS]
            ref[y + RADIUS, :, LANES - RADIUS :] = sides[lo : lo + n, RADIUS:]
        return carry

    lax.fori_loop(0, rows, fill, 0)
    b_hi, b_lo = split_bf16(bal_ref[...])
    srcs = [p_ref, a_ref, b_ref, a_ref]
    dsts = [a_ref, b_ref, a_ref, None]
    for p in range(PASSES):
        src = srcs[p]
        dst = dsts[p]

        def row(y, carry, src=src, dst=dst):
            srows = [s_ref[y - dy] for dy in (-1, 0, 1)]
            coefs = {}
            for dy in (-1, 0, 1):
                for dx in (-1, 0, 1):
                    k = (dy + 1) * 3 + dx + 1
                    coefs[(dy, dx)] = jnp.broadcast_to(
                        srows[dy + 1][k : k + 1, :], (CHUNK, LANES)
                    )
            depth = jnp.broadcast_to(srows[1][9:10, :], (CHUNK, LANES))
            for c0 in range(0, chans, CHUNK):
                sums = [None, None, None]
                for dy in (-1, 0, 1):
                    v = src[y - dy, c0 : c0 + CHUNK, :]
                    for dx in (-1, 0, 1):
                        t = coefs[(dy, dx)] * v
                        sums[dx + 1] = t if sums[dx + 1] is None else sums[dx + 1] + t
                acc = (
                    sums[1]
                    + pltpu.roll(sums[0], LANES - 1, 1)
                    + pltpu.roll(sums[2], 1, 1)
                )
                u_ref[c0 : c0 + CHUNK, :] = jnp.where(
                    lvl_ref[c0 : c0 + CHUNK, :] < depth, acc, 0.0
                )
            u_hi, u_lo = split_bf16(u_ref[...])
            res = jnp.dot(b_hi, u_hi, preferred_element_type=jnp.float32)
            res = res + jnp.dot(b_hi, u_lo, preferred_element_type=jnp.float32)
            res = res + jnp.dot(b_lo, u_hi, preferred_element_type=jnp.float32)
            if dst is None:
                out_ref[y - RADIUS] = res[:out_ch, :cols]
            else:
                dst[y] = res
            return carry

        lax.fori_loop(p + 1, full - 1 - p, row, 0, unroll=2)


def run_passes(field, halos, balance, chans):
    rows, cols, cpad = field.shape
    full = rows + 2 * RADIUS
    gap = LANES - cols - 2 * RADIUS
    ew = jnp.concatenate([halos["east"], halos["west"]], axis=1)
    top = jnp.concatenate([halos["south"], side_lanes(halos["se"], halos["sw"], gap)], axis=2)
    bot = jnp.concatenate([halos["north"], side_lanes(halos["ne"], halos["nw"], gap)], axis=2)
    lvl = jnp.broadcast_to(
        (jnp.arange(CPAD) % LEVELS).astype(jnp.float32)[:, None], (CPAD, LANES)
    )
    bal_t = jnp.pad(balance.T, ((0, CPAD - chans), (0, CPAD - chans)))
    vmem = pltpu.VMEM
    work = full * CPAD * LANES
    return pl.pallas_call(
        passes_kernel,
        out_shape=jax.ShapeDtypeStruct((rows, chans, cols), jnp.float32),
        in_specs=[pl.BlockSpec(memory_space=vmem)] * 6,
        out_specs=pl.BlockSpec(memory_space=vmem),
        scratch_shapes=[
            vmem((full, CPAD, LANES), jnp.float32),
            vmem((full, CPAD, LANES), jnp.float32),
            vmem((full, CPAD, LANES), jnp.float32),
            vmem((full, SPAD, LANES), jnp.float32),
            vmem((CPAD, LANES), jnp.float32),
        ],
        compiler_params=pltpu.CompilerParams(vmem_limit_bytes=62 * 1024 * 1024),
        cost_estimate=pl.CostEstimate(
            flops=PASSES * (work * 20 + 6 * full * CPAD * CPAD * LANES),
            bytes_accessed=4 * (work + rows * chans * cols),
            transcendentals=0,
        ),
    )(field, ew, top, bot, lvl, bal_t)


def local(innovations, owner_tile, obs_column, obs_depth, coefficients, sea_depth, balance):
    channels = innovations.shape[0]
    obs_count = innovations.shape[1]
    devices = lax.axis_size("lon") * lax.axis_size("lat")
    capacity = 4 * obs_count // devices
    rows_y = sea_depth.shape[0]
    cols_x = sea_depth.shape[1]

    stat = jnp.concatenate([coefficients, sea_depth.astype(jnp.float32)[None]], axis=0)
    stat = jnp.transpose(stat, (1, 2, 0)).reshape(rows_y * cols_x, stat.shape[0])
    base = jnp.concatenate(
        [
            jnp.zeros((rows_y * cols_x, CPAD), jnp.float32),
            stat,
            jnp.zeros((rows_y * cols_x, SPAD - stat.shape[1]), jnp.float32),
        ],
        axis=1,
    )

    level_ids = jnp.arange(channels) % LEVELS
    kept = jnp.where(level_ids[:, None] < obs_depth[None, :], innovations, 0.0)
    targets = owner_tile[:, 0]
    one_hot = (targets[:, None] == jnp.arange(devices, dtype=jnp.int32)[None, :]).astype(jnp.int32)
    before = jnp.cumsum(one_hot, axis=0) - one_hot
    slot_rank = jnp.sum(before * one_hot, axis=1)
    destination = targets * capacity + slot_rank
    payload = jnp.concatenate(
        [
            kept.T,
            jnp.zeros((obs_count, CPAD - channels - 1), jnp.float32),
            obs_column.astype(jnp.float32)[:, None],
        ],
        axis=1,
    )
    send = jnp.zeros((devices * capacity, CPAD), jnp.float32).at[destination].set(payload)
    got = lax.all_to_all(
        send.reshape(devices, capacity, CPAD), ("lon", "lat"), 0, 0, tiled=True
    ).reshape(devices * capacity, CPAD)
    where = got[:, CPAD - 1].astype(jnp.int32)
    field = base.at[where, :CPAD].add(got)
    field = field.reshape(rows_y, cols_x, CPAD + SPAD)
    out = run_passes(field, field_halos(field), balance, channels)
    return jnp.transpose(out, (1, 0, 2))


def solution(mesh):
    placed = (
        P(None, ("lon", "lat")),
        P(("lon", "lat"), None),
        P(("lon", "lat")),
        P(("lon", "lat")),
        P(None, "lat", "lon"),
        P("lat", "lon"),
        P(),
    )
    return jax.shard_map(
        local, mesh=mesh, in_specs=placed, out_specs=P(None, "lat", "lon"), check_vma=False
    )
```

```python
import jax
import jax.numpy as jnp
from jax import lax
from jax.experimental import pallas as pl
from jax.experimental.pallas import tpu as pltpu
from jax.sharding import PartitionSpec as P

LEVELS = 75
PASSES = 4
RADIUS = PASSES
LANES = 256
CPAD = 152
CHUNK = 8
SPAD = 16


def shift_lon(block, step):
    count = lax.axis_size("lon")
    return lax.ppermute(block, "lon", [(i, (i + step) % count) for i in range(count)])


def shift_lat(block, step):
    count = lax.axis_size("lat")
    return lax.ppermute(
        block, "lat", [(i, i + step) for i in range(count) if 0 <= i + step < count]
    )


def shift_both(block, step_lon, step_lat):
    n_lon = lax.axis_size("lon")
    n_lat = lax.axis_size("lat")
    pairs = []
    for i in range(n_lon):
        for j in range(n_lat):
            if 0 <= j + step_lat < n_lat:
                pairs.append((i * n_lat + j, ((i + step_lon) % n_lon) * n_lat + j + step_lat))
    return lax.ppermute(block, ("lon", "lat"), pairs)


DIRECTIONS = (
    ("west", lambda v, r: v[:, :, v.shape[2] - r :], "lon", 1, 0),
    ("east", lambda v, r: v[:, :, :r], "lon", -1, 0),
    ("south", lambda v, r: v[v.shape[0] - r :], "lat", 0, 1),
    ("north", lambda v, r: v[:r], "lat", 0, -1),
    ("sw", lambda v, r: v[v.shape[0] - r :, :, v.shape[2] - r :], "both", 1, 1),
    ("se", lambda v, r: v[v.shape[0] - r :, :, :r], "both", -1, 1),
    ("nw", lambda v, r: v[:r, :, v.shape[2] - r :], "both", 1, -1),
    ("ne", lambda v, r: v[:r, :, :r], "both", -1, -1),
)


def exchange(parts):
    got = [dict() for _ in parts]
    for name, take, axis, step_lon, step_lat in DIRECTIONS:
        pieces = [take(v, RADIUS) for v in parts]
        flat = jnp.concatenate([p.reshape(-1) for p in pieces])
        if axis == "lon":
            flat = shift_lon(flat, step_lon)
        elif axis == "lat":
            flat = shift_lat(flat, step_lat)
        else:
            flat = shift_both(flat, step_lon, step_lat)
        offset = 0
        for i, p in enumerate(pieces):
            got[i][name] = flat[offset : offset + p.size].reshape(p.shape)
            offset += p.size
    return got


def field_halos(f):
    rows, cols, _ = f.shape
    r = RADIUS
    v_top = jnp.transpose(f[:r], (0, 2, 1))
    v_bot = jnp.transpose(f[rows - r :], (0, 2, 1))

    def t(a):
        return jnp.transpose(a, (0, 2, 1))

    return {
        "west": shift_lon(f[:, cols - r :, :], 1),
        "east": shift_lon(f[:, :r, :], -1),
        "south": shift_lat(v_bot, 1),
        "north": shift_lat(v_top, -1),
        "sw": t(shift_both(f[rows - r :, cols - r :, :], 1, 1)),
        "se": t(shift_both(f[rows - r :, :r, :], -1, 1)),
        "nw": t(shift_both(f[:r, cols - r :, :], 1, -1)),
        "ne": t(shift_both(f[:r, :r, :], -1, -1)),
    }


def side_lanes(east, west, gap):
    zeros = jnp.zeros(east.shape[:2] + (gap,), jnp.float32)
    return jnp.concatenate([east, zeros, west], axis=2)


def assemble(v, h):
    cols = v.shape[2]
    gap = LANES - cols - 2 * RADIUS
    top = jnp.concatenate([h["south"], side_lanes(h["se"], h["sw"], gap)], axis=2)
    mid = jnp.concatenate([v, side_lanes(h["east"], h["west"], gap)], axis=2)
    bot = jnp.concatenate([h["north"], side_lanes(h["ne"], h["nw"], gap)], axis=2)
    return jnp.concatenate([top, mid, bot], axis=0)


def split_bf16(x):
    hi = x.astype(jnp.bfloat16)
    lo = (x - hi.astype(jnp.float32)).astype(jnp.bfloat16)
    return hi, lo


def passes_kernel(
    v_ref, ew_ref, top_ref, bot_ref, lvl_ref, bal_ref, out_ref, a_ref, b_ref, p_ref, s_ref, u_ref
):
    full = p_ref.shape[0]
    rows = v_ref.shape[0]
    cols = v_ref.shape[1]
    chans = p_ref.shape[1]
    out_ch = out_ref.shape[1]
    statc = s_ref.shape[1]
    p_ref[:RADIUS] = top_ref[:, :chans, :]
    s_ref[:RADIUS] = top_ref[:, chans:, :]
    p_ref[full - RADIUS :] = bot_ref[:, :chans, :]
    s_ref[full - RADIUS :] = bot_ref[:, chans:, :]

    def fill(y, carry):
        body = jnp.transpose(v_ref[y])
        sides = jnp.transpose(ew_ref[y])
        for ref, lo, n in ((p_ref, 0, chans), (s_ref, chans, statc)):
            ref[y + RADIUS, :, :cols] = body[lo : lo + n]
            ref[y + RADIUS, :, cols:] = jnp.zeros((n, LANES - cols), jnp.float32)
            ref[y + RADIUS, :, cols : cols + RADIUS] = sides[lo : lo + n, :RADIUS]
            ref[y + RADIUS, :, LANES - RADIUS :] = sides[lo : lo + n, RADIUS:]
        return carry

    lax.fori_loop(0, rows, fill, 0)
    b_hi, b_lo = split_bf16(bal_ref[...])
    srcs = [p_ref, a_ref, b_ref, a_ref]
    dsts = [a_ref, b_ref, a_ref, None]
    for p in range(PASSES):
        src = srcs[p]
        dst = dsts[p]

        def row(y, carry, src=src, dst=dst):
            srows = [s_ref[y - dy] for dy in (-1, 0, 1)]
            coefs = {}
            for dy in (-1, 0, 1):
                for dx in (-1, 0, 1):
                    k = (dy + 1) * 3 + dx + 1
                    coefs[(dy, dx)] = jnp.broadcast_to(
                        srows[dy + 1][k : k + 1, :], (CHUNK, LANES)
                    )
            depth = jnp.broadcast_to(srows[1][9:10, :], (CHUNK, LANES))
            for c0 in range(0, chans, CHUNK):
                sums = [None, None, None]
                for dy in (-1, 0, 1):
                    v = src[y - dy, c0 : c0 + CHUNK, :]
                    for dx in (-1, 0, 1):
                        t = coefs[(dy, dx)] * v
                        sums[dx + 1] = t if sums[dx + 1] is None else sums[dx + 1] + t
                acc = (
                    sums[1]
                    + pltpu.roll(sums[0], LANES - 1, 1)
                    + pltpu.roll(sums[2], 1, 1)
                )
                u_ref[c0 : c0 + CHUNK, :] = jnp.where(
                    lvl_ref[c0 : c0 + CHUNK, :] < depth, acc, 0.0
                )
            u_hi, u_lo = split_bf16(u_ref[...])
            res = jnp.dot(b_hi, u_hi, preferred_element_type=jnp.float32)
            res = res + jnp.dot(b_hi, u_lo, preferred_element_type=jnp.float32)
            res = res + jnp.dot(b_lo, u_hi, preferred_element_type=jnp.float32)
            if dst is None:
                out_ref[y - RADIUS] = res[:out_ch, :cols]
            else:
                dst[y] = res
            return carry

        lax.fori_loop(p + 1, full - 1 - p, row, 0, unroll=2)


def run_passes(field, halos, balance, chans):
    rows, cols, cpad = field.shape
    full = rows + 2 * RADIUS
    gap = LANES - cols - 2 * RADIUS
    ew = jnp.concatenate([halos["east"], halos["west"]], axis=1)
    top = jnp.concatenate([halos["south"], side_lanes(halos["se"], halos["sw"], gap)], axis=2)
    bot = jnp.concatenate([halos["north"], side_lanes(halos["ne"], halos["nw"], gap)], axis=2)
    lvl = jnp.broadcast_to(
        (jnp.arange(CPAD) % LEVELS).astype(jnp.float32)[:, None], (CPAD, LANES)
    )
    bal_t = jnp.pad(balance.T, ((0, CPAD - chans), (0, CPAD - chans)))
    vmem = pltpu.VMEM
    work = full * CPAD * LANES
    return pl.pallas_call(
        passes_kernel,
        out_shape=jax.ShapeDtypeStruct((rows, chans, cols), jnp.float32),
        in_specs=[pl.BlockSpec(memory_space=vmem)] * 6,
        out_specs=pl.BlockSpec(memory_space=vmem),
        scratch_shapes=[
            vmem((full, CPAD, LANES), jnp.float32),
            vmem((full, CPAD, LANES), jnp.float32),
            vmem((full, CPAD, LANES), jnp.float32),
            vmem((full, SPAD, LANES), jnp.float32),
            vmem((CPAD, LANES), jnp.float32),
        ],
        compiler_params=pltpu.CompilerParams(vmem_limit_bytes=62 * 1024 * 1024),
        cost_estimate=pl.CostEstimate(
            flops=PASSES * (work * 20 + 6 * full * CPAD * CPAD * LANES),
            bytes_accessed=4 * (work + rows * chans * cols),
            transcendentals=0,
        ),
    )(field, ew, top, bot, lvl, bal_t)


def local(innovations, owner_tile, obs_column, obs_depth, coefficients, sea_depth, balance):
    channels = innovations.shape[0]
    obs_count = innovations.shape[1]
    devices = lax.axis_size("lon") * lax.axis_size("lat")
    capacity = 4 * obs_count // devices
    rows_y = sea_depth.shape[0]
    cols_x = sea_depth.shape[1]

    stat = jnp.concatenate([coefficients, sea_depth.astype(jnp.float32)[None]], axis=0)
    stat = jnp.transpose(stat, (1, 2, 0)).reshape(rows_y * cols_x, stat.shape[0])
    base = jnp.concatenate(
        [
            jnp.zeros((rows_y * cols_x, CPAD), jnp.float32),
            stat,
            jnp.zeros((rows_y * cols_x, SPAD - stat.shape[1]), jnp.float32),
        ],
        axis=1,
    )

    level_ids = jnp.arange(channels) % LEVELS
    kept = jnp.where(level_ids[:, None] < obs_depth[None, :], innovations, 0.0)
    targets = owner_tile[:, 0]
    one_hot = (targets[:, None] == jnp.arange(devices, dtype=jnp.int32)[None, :]).astype(jnp.int32)
    before = jnp.cumsum(one_hot, axis=0) - one_hot
    slot_rank = jnp.sum(before * one_hot, axis=1)
    destination = targets * capacity + slot_rank
    payload = jnp.concatenate(
        [
            kept.T,
            jnp.zeros((obs_count, CPAD - channels - 1), jnp.float32),
            obs_column.astype(jnp.float32)[:, None],
        ],
        axis=1,
    )
    send = jnp.zeros((devices * capacity, CPAD), jnp.float32).at[destination].set(payload)
    got = lax.all_to_all(
        send.reshape(devices, capacity, CPAD), ("lon", "lat"), 0, 0, tiled=True
    ).reshape(devices * capacity, CPAD)
    where = got[:, CPAD - 1].astype(jnp.int32)
    got = jnp.pad(got, ((0, 0), (0, SPAD)))
    field = base.at[where].add(got)
    field = field.reshape(rows_y, cols_x, CPAD + SPAD)
    out = run_passes(field, field_halos(field), balance, channels)
    return jnp.transpose(out, (1, 0, 2))


def solution(mesh):
    placed = (
        P(None, ("lon", "lat")),
        P(("lon", "lat"), None),
        P(("lon", "lat")),
        P(("lon", "lat")),
        P(None, "lat", "lon"),
        P("lat", "lon"),
        P(),
    )
    return jax.shard_map(
        local, mesh=mesh, in_specs=placed, out_specs=P(None, "lat", "lon"), check_vma=False
    )
```

```python
import jax
import jax.numpy as jnp
from jax import lax
from jax.experimental import pallas as pl
from jax.experimental.pallas import tpu as pltpu
from jax.sharding import PartitionSpec as P

LEVELS = 75
PASSES = 4
RADIUS = PASSES
LANES = 256
CPAD = 152
CHUNK = 8
SPAD = 16


def shift_lon(block, step):
    count = lax.axis_size("lon")
    return lax.ppermute(block, "lon", [(i, (i + step) % count) for i in range(count)])


def shift_lat(block, step):
    count = lax.axis_size("lat")
    return lax.ppermute(
        block, "lat", [(i, i + step) for i in range(count) if 0 <= i + step < count]
    )


def shift_both(block, step_lon, step_lat):
    n_lon = lax.axis_size("lon")
    n_lat = lax.axis_size("lat")
    pairs = []
    for i in range(n_lon):
        for j in range(n_lat):
            if 0 <= j + step_lat < n_lat:
                pairs.append((i * n_lat + j, ((i + step_lon) % n_lon) * n_lat + j + step_lat))
    return lax.ppermute(block, ("lon", "lat"), pairs)


DIRECTIONS = (
    ("west", lambda v, r: v[:, :, v.shape[2] - r :], "lon", 1, 0),
    ("east", lambda v, r: v[:, :, :r], "lon", -1, 0),
    ("south", lambda v, r: v[v.shape[0] - r :], "lat", 0, 1),
    ("north", lambda v, r: v[:r], "lat", 0, -1),
    ("sw", lambda v, r: v[v.shape[0] - r :, :, v.shape[2] - r :], "both", 1, 1),
    ("se", lambda v, r: v[v.shape[0] - r :, :, :r], "both", -1, 1),
    ("nw", lambda v, r: v[:r, :, v.shape[2] - r :], "both", 1, -1),
    ("ne", lambda v, r: v[:r, :, :r], "both", -1, -1),
)


def exchange(parts):
    got = [dict() for _ in parts]
    for name, take, axis, step_lon, step_lat in DIRECTIONS:
        pieces = [take(v, RADIUS) for v in parts]
        flat = jnp.concatenate([p.reshape(-1) for p in pieces])
        if axis == "lon":
            flat = shift_lon(flat, step_lon)
        elif axis == "lat":
            flat = shift_lat(flat, step_lat)
        else:
            flat = shift_both(flat, step_lon, step_lat)
        offset = 0
        for i, p in enumerate(pieces):
            got[i][name] = flat[offset : offset + p.size].reshape(p.shape)
            offset += p.size
    return got


def field_halos(f):
    rows, cols, _ = f.shape
    r = RADIUS
    v_top = jnp.transpose(f[:r], (0, 2, 1))
    v_bot = jnp.transpose(f[rows - r :], (0, 2, 1))

    def t(a):
        return jnp.transpose(a, (0, 2, 1))

    return {
        "west": shift_lon(f[:, cols - r :, :], 1),
        "east": shift_lon(f[:, :r, :], -1),
        "south": shift_lat(v_bot, 1),
        "north": shift_lat(v_top, -1),
        "sw": t(shift_both(f[rows - r :, cols - r :, :], 1, 1)),
        "se": t(shift_both(f[rows - r :, :r, :], -1, 1)),
        "nw": t(shift_both(f[:r, cols - r :, :], 1, -1)),
        "ne": t(shift_both(f[:r, :r, :], -1, -1)),
    }


def side_lanes(east, west, gap):
    zeros = jnp.zeros(east.shape[:2] + (gap,), jnp.float32)
    return jnp.concatenate([east, zeros, west], axis=2)


def assemble(v, h):
    cols = v.shape[2]
    gap = LANES - cols - 2 * RADIUS
    top = jnp.concatenate([h["south"], side_lanes(h["se"], h["sw"], gap)], axis=2)
    mid = jnp.concatenate([v, side_lanes(h["east"], h["west"], gap)], axis=2)
    bot = jnp.concatenate([h["north"], side_lanes(h["ne"], h["nw"], gap)], axis=2)
    return jnp.concatenate([top, mid, bot], axis=0)


def split_bf16(x):
    hi = x.astype(jnp.bfloat16)
    lo = (x - hi.astype(jnp.float32)).astype(jnp.bfloat16)
    return hi, lo


def passes_kernel(
    v_ref, ew_ref, top_ref, bot_ref, lvl_ref, bal_ref, out_ref, a_ref, b_ref, p_ref, s_ref, u_ref
):
    full = p_ref.shape[0]
    rows = v_ref.shape[0]
    cols = v_ref.shape[1]
    chans = p_ref.shape[1]
    out_ch = out_ref.shape[1]
    statc = s_ref.shape[1]
    p_ref[:RADIUS] = top_ref[:, :chans, :]
    s_ref[:RADIUS] = top_ref[:, chans:, :]
    p_ref[full - RADIUS :] = bot_ref[:, :chans, :]
    s_ref[full - RADIUS :] = bot_ref[:, chans:, :]

    def fill(y, carry):
        body = jnp.transpose(v_ref[y])
        sides = jnp.transpose(ew_ref[y])
        for ref, lo, n in ((p_ref, 0, chans), (s_ref, chans, statc)):
            ref[y + RADIUS, :, :cols] = body[lo : lo + n]
            ref[y + RADIUS, :, cols:] = jnp.zeros((n, LANES - cols), jnp.float32)
            ref[y + RADIUS, :, cols : cols + RADIUS] = sides[lo : lo + n, :RADIUS]
            ref[y + RADIUS, :, LANES - RADIUS :] = sides[lo : lo + n, RADIUS:]
        return carry

    lax.fori_loop(0, rows, fill, 0)
    b_hi, b_lo = split_bf16(bal_ref[...])
    srcs = [p_ref, a_ref, b_ref, a_ref]
    dsts = [a_ref, b_ref, a_ref, None]
    for p in range(PASSES):
        src = srcs[p]
        dst = dsts[p]

        def row(y, carry, src=src, dst=dst):
            srows = [s_ref[y - dy] for dy in (-1, 0, 1)]
            coefs = {}
            for dy in (-1, 0, 1):
                for dx in (-1, 0, 1):
                    k = (dy + 1) * 3 + dx + 1
                    coefs[(dy, dx)] = jnp.broadcast_to(
                        srows[dy + 1][k : k + 1, :], (CHUNK, LANES)
                    )
            depth = jnp.broadcast_to(srows[1][9:10, :], (CHUNK, LANES))
            for c0 in range(0, chans, CHUNK):
                sums = [None, None, None]
                for dy in (-1, 0, 1):
                    v = src[y - dy, c0 : c0 + CHUNK, :]
                    for dx in (-1, 0, 1):
                        t = coefs[(dy, dx)] * v
                        sums[dx + 1] = t if sums[dx + 1] is None else sums[dx + 1] + t
                acc = (
                    sums[1]
                    + pltpu.roll(sums[0], LANES - 1, 1)
                    + pltpu.roll(sums[2], 1, 1)
                )
                u_ref[c0 : c0 + CHUNK, :] = jnp.where(
                    lvl_ref[c0 : c0 + CHUNK, :] < depth, acc, 0.0
                )
            u_hi, u_lo = split_bf16(u_ref[...])
            res = jnp.dot(b_hi, u_hi, preferred_element_type=jnp.float32)
            res = res + jnp.dot(b_hi, u_lo, preferred_element_type=jnp.float32)
            res = res + jnp.dot(b_lo, u_hi, preferred_element_type=jnp.float32)
            if dst is None:
                out_ref[y - RADIUS] = res[:out_ch, :cols]
            else:
                dst[y] = res
            return carry

        lax.fori_loop(p + 1, full - 1 - p, row, 0, unroll=2)


def run_passes(field, halos, balance, chans):
    rows, cols, cpad = field.shape
    full = rows + 2 * RADIUS
    gap = LANES - cols - 2 * RADIUS
    ew = jnp.concatenate([halos["east"], halos["west"]], axis=1)
    top = jnp.concatenate([halos["south"], side_lanes(halos["se"], halos["sw"], gap)], axis=2)
    bot = jnp.concatenate([halos["north"], side_lanes(halos["ne"], halos["nw"], gap)], axis=2)
    lvl = jnp.broadcast_to(
        (jnp.arange(CPAD) % LEVELS).astype(jnp.float32)[:, None], (CPAD, LANES)
    )
    bal_t = jnp.pad(balance.T, ((0, CPAD - chans), (0, CPAD - chans)))
    vmem = pltpu.VMEM
    work = full * CPAD * LANES
    return pl.pallas_call(
        passes_kernel,
        out_shape=jax.ShapeDtypeStruct((rows, chans, cols), jnp.float32),
        in_specs=[pl.BlockSpec(memory_space=vmem)] * 6,
        out_specs=pl.BlockSpec(memory_space=vmem),
        scratch_shapes=[
            vmem((full, CPAD, LANES), jnp.float32),
            vmem((full, CPAD, LANES), jnp.float32),
            vmem((full, CPAD, LANES), jnp.float32),
            vmem((full, SPAD, LANES), jnp.float32),
            vmem((CPAD, LANES), jnp.float32),
        ],
        compiler_params=pltpu.CompilerParams(vmem_limit_bytes=62 * 1024 * 1024),
        cost_estimate=pl.CostEstimate(
            flops=PASSES * (work * 20 + 6 * full * CPAD * CPAD * LANES),
            bytes_accessed=4 * (work + rows * chans * cols),
            transcendentals=0,
        ),
    )(field, ew, top, bot, lvl, bal_t)


def local(innovations, owner_tile, obs_column, obs_depth, coefficients, sea_depth, balance):
    channels = innovations.shape[0]
    obs_count = innovations.shape[1]
    devices = lax.axis_size("lon") * lax.axis_size("lat")
    capacity = 4 * obs_count // devices
    rows_y = sea_depth.shape[0]
    cols_x = sea_depth.shape[1]

    stat = jnp.concatenate([coefficients, sea_depth.astype(jnp.float32)[None]], axis=0)
    stat = jnp.transpose(stat, (1, 2, 0)).reshape(rows_y * cols_x, stat.shape[0])
    base = jnp.concatenate(
        [
            jnp.zeros((rows_y * cols_x, CPAD), jnp.float32),
            stat,
            jnp.zeros((rows_y * cols_x, SPAD - stat.shape[1]), jnp.float32),
        ],
        axis=1,
    )

    level_ids = jnp.arange(channels) % LEVELS
    kept = jnp.where(level_ids[:, None] < obs_depth[None, :], innovations, 0.0)
    targets = owner_tile[:, 0]
    one_hot = (targets[:, None] == jnp.arange(devices, dtype=jnp.int32)[None, :]).astype(jnp.int32)
    before = jnp.cumsum(one_hot, axis=0) - one_hot
    slot_rank = jnp.sum(before * one_hot, axis=1)
    destination = targets * capacity + slot_rank
    payload = jnp.concatenate(
        [
            kept.T,
            jnp.zeros((obs_count, CPAD - channels - 1), jnp.float32),
            obs_column.astype(jnp.float32)[:, None],
        ],
        axis=1,
    )
    send = jnp.zeros((devices * capacity, CPAD), jnp.float32).at[destination].set(payload)
    block = capacity * CPAD
    shape = (devices, block // 128, 128) if block % 128 == 0 else (devices, capacity, CPAD)
    got = lax.all_to_all(send.reshape(shape), ("lon", "lat"), 0, 0, tiled=True).reshape(
        devices * capacity, CPAD
    )
    where = got[:, CPAD - 1].astype(jnp.int32)
    got = jnp.pad(got, ((0, 0), (0, SPAD)))
    field = base.at[where].add(got)
    field = field.reshape(rows_y, cols_x, CPAD + SPAD)
    out = run_passes(field, field_halos(field), balance, channels)
    return jnp.transpose(out, (1, 0, 2))


def solution(mesh):
    placed = (
        P(None, ("lon", "lat")),
        P(("lon", "lat"), None),
        P(("lon", "lat")),
        P(("lon", "lat")),
        P(None, "lat", "lon"),
        P("lat", "lon"),
        P(),
    )
    return jax.shard_map(
        local, mesh=mesh, in_specs=placed, out_specs=P(None, "lat", "lon"), check_vma=False
    )
```

```python
import jax
import jax.numpy as jnp
from jax import lax
from jax.experimental import pallas as pl
from jax.experimental.pallas import tpu as pltpu
from jax.sharding import PartitionSpec as P

LEVELS = 75
PASSES = 4
RADIUS = PASSES
LANES = 256
CPAD = 152
CHUNK = 8
SPAD = 16


def shift_lon(block, step):
    count = lax.axis_size("lon")
    return lax.ppermute(block, "lon", [(i, (i + step) % count) for i in range(count)])


def shift_lat(block, step):
    count = lax.axis_size("lat")
    return lax.ppermute(
        block, "lat", [(i, i + step) for i in range(count) if 0 <= i + step < count]
    )


def shift_both(block, step_lon, step_lat):
    n_lon = lax.axis_size("lon")
    n_lat = lax.axis_size("lat")
    pairs = []
    for i in range(n_lon):
        for j in range(n_lat):
            if 0 <= j + step_lat < n_lat:
                pairs.append((i * n_lat + j, ((i + step_lon) % n_lon) * n_lat + j + step_lat))
    return lax.ppermute(block, ("lon", "lat"), pairs)


DIRECTIONS = (
    ("west", lambda v, r: v[:, :, v.shape[2] - r :], "lon", 1, 0),
    ("east", lambda v, r: v[:, :, :r], "lon", -1, 0),
    ("south", lambda v, r: v[v.shape[0] - r :], "lat", 0, 1),
    ("north", lambda v, r: v[:r], "lat", 0, -1),
    ("sw", lambda v, r: v[v.shape[0] - r :, :, v.shape[2] - r :], "both", 1, 1),
    ("se", lambda v, r: v[v.shape[0] - r :, :, :r], "both", -1, 1),
    ("nw", lambda v, r: v[:r, :, v.shape[2] - r :], "both", 1, -1),
    ("ne", lambda v, r: v[:r, :, :r], "both", -1, -1),
)


def exchange(parts):
    got = [dict() for _ in parts]
    for name, take, axis, step_lon, step_lat in DIRECTIONS:
        pieces = [take(v, RADIUS) for v in parts]
        flat = jnp.concatenate([p.reshape(-1) for p in pieces])
        if axis == "lon":
            flat = shift_lon(flat, step_lon)
        elif axis == "lat":
            flat = shift_lat(flat, step_lat)
        else:
            flat = shift_both(flat, step_lon, step_lat)
        offset = 0
        for i, p in enumerate(pieces):
            got[i][name] = flat[offset : offset + p.size].reshape(p.shape)
            offset += p.size
    return got


def field_halos(f):
    rows, cols, _ = f.shape
    r = RADIUS
    v_top = jnp.transpose(f[:r], (0, 2, 1))
    v_bot = jnp.transpose(f[rows - r :], (0, 2, 1))

    def t(a):
        return jnp.transpose(a, (0, 2, 1))

    return {
        "west": shift_lon(f[:, cols - r :, :], 1),
        "east": shift_lon(f[:, :r, :], -1),
        "south": shift_lat(v_bot, 1),
        "north": shift_lat(v_top, -1),
        "sw": t(shift_both(f[rows - r :, cols - r :, :], 1, 1)),
        "se": t(shift_both(f[rows - r :, :r, :], -1, 1)),
        "nw": t(shift_both(f[:r, cols - r :, :], 1, -1)),
        "ne": t(shift_both(f[:r, :r, :], -1, -1)),
    }


def side_lanes(east, west, gap):
    zeros = jnp.zeros(east.shape[:2] + (gap,), jnp.float32)
    return jnp.concatenate([east, zeros, west], axis=2)


def assemble(v, h):
    cols = v.shape[2]
    gap = LANES - cols - 2 * RADIUS
    top = jnp.concatenate([h["south"], side_lanes(h["se"], h["sw"], gap)], axis=2)
    mid = jnp.concatenate([v, side_lanes(h["east"], h["west"], gap)], axis=2)
    bot = jnp.concatenate([h["north"], side_lanes(h["ne"], h["nw"], gap)], axis=2)
    return jnp.concatenate([top, mid, bot], axis=0)


def split_bf16(x):
    hi = x.astype(jnp.bfloat16)
    lo = (x - hi.astype(jnp.float32)).astype(jnp.bfloat16)
    return hi, lo


def passes_kernel(
    v_ref, ew_ref, top_ref, bot_ref, lvl_ref, bal_ref, out_ref, a_ref, b_ref, p_ref, s_ref, u_ref
):
    full = p_ref.shape[0]
    rows = v_ref.shape[0]
    cols = v_ref.shape[1]
    chans = p_ref.shape[1]
    out_ch = out_ref.shape[1]
    statc = s_ref.shape[1]
    p_ref[:RADIUS] = top_ref[:, :chans, :]
    s_ref[:RADIUS] = top_ref[:, chans:, :]
    p_ref[full - RADIUS :] = bot_ref[:, :chans, :]
    s_ref[full - RADIUS :] = bot_ref[:, chans:, :]

    def fill(y, carry):
        body = jnp.transpose(v_ref[y])
        sides = jnp.transpose(ew_ref[y])
        for ref, lo, n in ((p_ref, 0, chans), (s_ref, chans, statc)):
            ref[y + RADIUS, :, :cols] = body[lo : lo + n]
            ref[y + RADIUS, :, cols:] = jnp.zeros((n, LANES - cols), jnp.float32)
            ref[y + RADIUS, :, cols : cols + RADIUS] = sides[lo : lo + n, :RADIUS]
            ref[y + RADIUS, :, LANES - RADIUS :] = sides[lo : lo + n, RADIUS:]
        return carry

    lax.fori_loop(0, rows, fill, 0, unroll=2)
    b_hi, b_lo = split_bf16(bal_ref[...])
    srcs = [p_ref, a_ref, b_ref, a_ref]
    dsts = [a_ref, b_ref, a_ref, None]
    for p in range(PASSES):
        src = srcs[p]
        dst = dsts[p]

        def row(y, carry, src=src, dst=dst):
            srows = [s_ref[y - dy] for dy in (-1, 0, 1)]
            coefs = {}
            for dy in (-1, 0, 1):
                for dx in (-1, 0, 1):
                    k = (dy + 1) * 3 + dx + 1
                    coefs[(dy, dx)] = jnp.broadcast_to(
                        srows[dy + 1][k : k + 1, :], (CHUNK, LANES)
                    )
            depth = jnp.broadcast_to(srows[1][9:10, :], (CHUNK, LANES))
            for c0 in range(0, chans, CHUNK):
                sums = [None, None, None]
                for dy in (-1, 0, 1):
                    v = src[y - dy, c0 : c0 + CHUNK, :]
                    for dx in (-1, 0, 1):
                        t = coefs[(dy, dx)] * v
                        sums[dx + 1] = t if sums[dx + 1] is None else sums[dx + 1] + t
                acc = (
                    sums[1]
                    + pltpu.roll(sums[0], LANES - 1, 1)
                    + pltpu.roll(sums[2], 1, 1)
                )
                u_ref[c0 : c0 + CHUNK, :] = jnp.where(
                    lvl_ref[c0 : c0 + CHUNK, :] < depth, acc, 0.0
                )
            u_hi, u_lo = split_bf16(u_ref[...])
            res = jnp.dot(b_hi, u_hi, preferred_element_type=jnp.float32)
            res = res + jnp.dot(b_hi, u_lo, preferred_element_type=jnp.float32)
            res = res + jnp.dot(b_lo, u_hi, preferred_element_type=jnp.float32)
            if dst is None:
                out_ref[y - RADIUS] = res[:out_ch, :cols]
            else:
                dst[y] = res
            return carry

        lax.fori_loop(p + 1, full - 1 - p, row, 0, unroll=4)


def run_passes(field, halos, balance, chans):
    rows, cols, cpad = field.shape
    full = rows + 2 * RADIUS
    gap = LANES - cols - 2 * RADIUS
    ew = jnp.concatenate([halos["east"], halos["west"]], axis=1)
    top = jnp.concatenate([halos["south"], side_lanes(halos["se"], halos["sw"], gap)], axis=2)
    bot = jnp.concatenate([halos["north"], side_lanes(halos["ne"], halos["nw"], gap)], axis=2)
    lvl = jnp.broadcast_to(
        (jnp.arange(CPAD) % LEVELS).astype(jnp.float32)[:, None], (CPAD, LANES)
    )
    bal_t = jnp.pad(balance.T, ((0, CPAD - chans), (0, CPAD - chans)))
    vmem = pltpu.VMEM
    work = full * CPAD * LANES
    return pl.pallas_call(
        passes_kernel,
        out_shape=jax.ShapeDtypeStruct((rows, chans, cols), jnp.float32),
        in_specs=[pl.BlockSpec(memory_space=vmem)] * 6,
        out_specs=pl.BlockSpec(memory_space=vmem),
        scratch_shapes=[
            vmem((full, CPAD, LANES), jnp.float32),
            vmem((full, CPAD, LANES), jnp.float32),
            vmem((full, CPAD, LANES), jnp.float32),
            vmem((full, SPAD, LANES), jnp.float32),
            vmem((CPAD, LANES), jnp.float32),
        ],
        compiler_params=pltpu.CompilerParams(vmem_limit_bytes=62 * 1024 * 1024),
        cost_estimate=pl.CostEstimate(
            flops=PASSES * (work * 20 + 6 * full * CPAD * CPAD * LANES),
            bytes_accessed=4 * (work + rows * chans * cols),
            transcendentals=0,
        ),
    )(field, ew, top, bot, lvl, bal_t)


def local(innovations, owner_tile, obs_column, obs_depth, coefficients, sea_depth, balance):
    channels = innovations.shape[0]
    obs_count = innovations.shape[1]
    devices = lax.axis_size("lon") * lax.axis_size("lat")
    capacity = 4 * obs_count // devices
    rows_y = sea_depth.shape[0]
    cols_x = sea_depth.shape[1]

    stat = jnp.concatenate([coefficients, sea_depth.astype(jnp.float32)[None]], axis=0)
    stat = jnp.transpose(stat, (1, 2, 0)).reshape(rows_y * cols_x, stat.shape[0])
    base = jnp.concatenate(
        [
            jnp.zeros((rows_y * cols_x, CPAD), jnp.float32),
            stat,
            jnp.zeros((rows_y * cols_x, SPAD - stat.shape[1]), jnp.float32),
        ],
        axis=1,
    )

    level_ids = jnp.arange(channels) % LEVELS
    kept = jnp.where(level_ids[:, None] < obs_depth[None, :], innovations, 0.0)
    targets = owner_tile[:, 0]
    one_hot = (targets[:, None] == jnp.arange(devices, dtype=jnp.int32)[None, :]).astype(jnp.int32)
    before = jnp.cumsum(one_hot, axis=0) - one_hot
    slot_rank = jnp.sum(before * one_hot, axis=1)
    destination = targets * capacity + slot_rank
    payload = jnp.concatenate(
        [
            kept.T,
            jnp.zeros((obs_count, CPAD - channels - 1), jnp.float32),
            obs_column.astype(jnp.float32)[:, None],
        ],
        axis=1,
    )
    send = jnp.zeros((devices * capacity, CPAD), jnp.float32).at[destination].set(payload)
    got = lax.all_to_all(
        send.reshape(devices, capacity, CPAD), ("lon", "lat"), 0, 0, tiled=True
    ).reshape(devices * capacity, CPAD)
    where = got[:, CPAD - 1].astype(jnp.int32)
    got = jnp.pad(got, ((0, 0), (0, SPAD)))
    field = base.at[where].add(got)
    field = field.reshape(rows_y, cols_x, CPAD + SPAD)
    out = run_passes(field, field_halos(field), balance, channels)
    return jnp.transpose(out, (1, 0, 2))


def solution(mesh):
    placed = (
        P(None, ("lon", "lat")),
        P(("lon", "lat"), None),
        P(("lon", "lat")),
        P(("lon", "lat")),
        P(None, "lat", "lon"),
        P("lat", "lon"),
        P(),
    )
    return jax.shard_map(
        local, mesh=mesh, in_specs=placed, out_specs=P(None, "lat", "lon"), check_vma=False
    )
```

```python
import jax
import jax.numpy as jnp
from jax import lax
from jax.experimental import pallas as pl
from jax.experimental.pallas import tpu as pltpu
from jax.sharding import PartitionSpec as P

LEVELS = 75
PASSES = 4
RADIUS = PASSES
LANES = 256
CPAD = 152
CHUNK = 8
SPAD = 16


def shift_lon(block, step):
    count = lax.axis_size("lon")
    return lax.ppermute(block, "lon", [(i, (i + step) % count) for i in range(count)])


def shift_lat(block, step):
    count = lax.axis_size("lat")
    return lax.ppermute(
        block, "lat", [(i, i + step) for i in range(count) if 0 <= i + step < count]
    )


def shift_both(block, step_lon, step_lat):
    n_lon = lax.axis_size("lon")
    n_lat = lax.axis_size("lat")
    pairs = []
    for i in range(n_lon):
        for j in range(n_lat):
            if 0 <= j + step_lat < n_lat:
                pairs.append((i * n_lat + j, ((i + step_lon) % n_lon) * n_lat + j + step_lat))
    return lax.ppermute(block, ("lon", "lat"), pairs)


DIRECTIONS = (
    ("west", lambda v, r: v[:, :, v.shape[2] - r :], "lon", 1, 0),
    ("east", lambda v, r: v[:, :, :r], "lon", -1, 0),
    ("south", lambda v, r: v[v.shape[0] - r :], "lat", 0, 1),
    ("north", lambda v, r: v[:r], "lat", 0, -1),
    ("sw", lambda v, r: v[v.shape[0] - r :, :, v.shape[2] - r :], "both", 1, 1),
    ("se", lambda v, r: v[v.shape[0] - r :, :, :r], "both", -1, 1),
    ("nw", lambda v, r: v[:r, :, v.shape[2] - r :], "both", 1, -1),
    ("ne", lambda v, r: v[:r, :, :r], "both", -1, -1),
)


def exchange(parts):
    got = [dict() for _ in parts]
    for name, take, axis, step_lon, step_lat in DIRECTIONS:
        pieces = [take(v, RADIUS) for v in parts]
        flat = jnp.concatenate([p.reshape(-1) for p in pieces])
        if axis == "lon":
            flat = shift_lon(flat, step_lon)
        elif axis == "lat":
            flat = shift_lat(flat, step_lat)
        else:
            flat = shift_both(flat, step_lon, step_lat)
        offset = 0
        for i, p in enumerate(pieces):
            got[i][name] = flat[offset : offset + p.size].reshape(p.shape)
            offset += p.size
    return got


def field_halos(f):
    rows, cols, _ = f.shape
    r = RADIUS
    v_top = jnp.transpose(f[:r], (0, 2, 1))
    v_bot = jnp.transpose(f[rows - r :], (0, 2, 1))

    def t(a):
        return jnp.transpose(a, (0, 2, 1))

    return {
        "west": shift_lon(f[:, cols - r :, :], 1),
        "east": shift_lon(f[:, :r, :], -1),
        "south": shift_lat(v_bot, 1),
        "north": shift_lat(v_top, -1),
        "sw": t(shift_both(f[rows - r :, cols - r :, :], 1, 1)),
        "se": t(shift_both(f[rows - r :, :r, :], -1, 1)),
        "nw": t(shift_both(f[:r, cols - r :, :], 1, -1)),
        "ne": t(shift_both(f[:r, :r, :], -1, -1)),
    }


def side_lanes(east, west, gap):
    zeros = jnp.zeros(east.shape[:2] + (gap,), jnp.float32)
    return jnp.concatenate([east, zeros, west], axis=2)


def assemble(v, h):
    cols = v.shape[2]
    gap = LANES - cols - 2 * RADIUS
    top = jnp.concatenate([h["south"], side_lanes(h["se"], h["sw"], gap)], axis=2)
    mid = jnp.concatenate([v, side_lanes(h["east"], h["west"], gap)], axis=2)
    bot = jnp.concatenate([h["north"], side_lanes(h["ne"], h["nw"], gap)], axis=2)
    return jnp.concatenate([top, mid, bot], axis=0)


def split_bf16(x):
    hi = x.astype(jnp.bfloat16)
    lo = (x - hi.astype(jnp.float32)).astype(jnp.bfloat16)
    return hi, lo


def passes_kernel(
    v_ref, ew_ref, top_ref, bot_ref, lvl_ref, bal_ref, out_ref, a_ref, b_ref, p_ref, s_ref, u_ref
):
    full = p_ref.shape[0]
    rows = v_ref.shape[0]
    cols = v_ref.shape[1]
    chans = p_ref.shape[1]
    out_ch = out_ref.shape[1]
    statc = s_ref.shape[1]
    p_ref[:RADIUS] = top_ref[:, :chans, :]
    s_ref[:RADIUS] = top_ref[:, chans:, :]
    p_ref[full - RADIUS :] = bot_ref[:, :chans, :]
    s_ref[full - RADIUS :] = bot_ref[:, chans:, :]

    def fill(y, carry):
        body = jnp.transpose(v_ref[y])
        sides = jnp.transpose(ew_ref[y])
        for ref, lo, n in ((p_ref, 0, chans), (s_ref, chans, statc)):
            ref[y + RADIUS, :, :cols] = body[lo : lo + n]
            ref[y + RADIUS, :, cols:] = jnp.zeros((n, LANES - cols), jnp.float32)
            ref[y + RADIUS, :, cols : cols + RADIUS] = sides[lo : lo + n, :RADIUS]
            ref[y + RADIUS, :, LANES - RADIUS :] = sides[lo : lo + n, RADIUS:]
        return carry

    lax.fori_loop(0, rows, fill, 0, unroll=4)
    b_hi, b_lo = split_bf16(bal_ref[...])
    srcs = [p_ref, a_ref, b_ref, a_ref]
    dsts = [a_ref, b_ref, a_ref, None]
    for p in range(PASSES):
        src = srcs[p]
        dst = dsts[p]

        def row(y, carry, src=src, dst=dst):
            srows = [s_ref[y - dy] for dy in (-1, 0, 1)]
            coefs = {}
            for dy in (-1, 0, 1):
                for dx in (-1, 0, 1):
                    k = (dy + 1) * 3 + dx + 1
                    coefs[(dy, dx)] = jnp.broadcast_to(
                        srows[dy + 1][k : k + 1, :], (CHUNK, LANES)
                    )
            depth = jnp.broadcast_to(srows[1][9:10, :], (CHUNK, LANES))
            for c0 in range(0, chans, CHUNK):
                sums = [None, None, None]
                for dy in (-1, 0, 1):
                    v = src[y - dy, c0 : c0 + CHUNK, :]
                    for dx in (-1, 0, 1):
                        t = coefs[(dy, dx)] * v
                        sums[dx + 1] = t if sums[dx + 1] is None else sums[dx + 1] + t
                acc = (
                    sums[1]
                    + pltpu.roll(sums[0], LANES - 1, 1)
                    + pltpu.roll(sums[2], 1, 1)
                )
                u_ref[c0 : c0 + CHUNK, :] = jnp.where(
                    lvl_ref[c0 : c0 + CHUNK, :] < depth, acc, 0.0
                )
            u_hi, u_lo = split_bf16(u_ref[...])
            res = jnp.dot(b_hi, u_hi, preferred_element_type=jnp.float32)
            res = res + jnp.dot(b_hi, u_lo, preferred_element_type=jnp.float32)
            res = res + jnp.dot(b_lo, u_hi, preferred_element_type=jnp.float32)
            if dst is None:
                out_ref[y - RADIUS] = res[:out_ch, :cols]
            else:
                dst[y] = res
            return carry

        lax.fori_loop(p + 1, full - 1 - p, row, 0, unroll=8)


def run_passes(field, halos, balance, chans):
    rows, cols, cpad = field.shape
    full = rows + 2 * RADIUS
    gap = LANES - cols - 2 * RADIUS
    ew = jnp.concatenate([halos["east"], halos["west"]], axis=1)
    top = jnp.concatenate([halos["south"], side_lanes(halos["se"], halos["sw"], gap)], axis=2)
    bot = jnp.concatenate([halos["north"], side_lanes(halos["ne"], halos["nw"], gap)], axis=2)
    lvl = jnp.broadcast_to(
        (jnp.arange(CPAD) % LEVELS).astype(jnp.float32)[:, None], (CPAD, LANES)
    )
    bal_t = jnp.pad(balance.T, ((0, CPAD - chans), (0, CPAD - chans)))
    vmem = pltpu.VMEM
    work = full * CPAD * LANES
    return pl.pallas_call(
        passes_kernel,
        out_shape=jax.ShapeDtypeStruct((rows, chans, cols), jnp.float32),
        in_specs=[pl.BlockSpec(memory_space=vmem)] * 6,
        out_specs=pl.BlockSpec(memory_space=vmem),
        scratch_shapes=[
            vmem((full, CPAD, LANES), jnp.float32),
            vmem((full, CPAD, LANES), jnp.float32),
            vmem((full, CPAD, LANES), jnp.float32),
            vmem((full, SPAD, LANES), jnp.float32),
            vmem((CPAD, LANES), jnp.float32),
        ],
        compiler_params=pltpu.CompilerParams(vmem_limit_bytes=62 * 1024 * 1024),
        cost_estimate=pl.CostEstimate(
            flops=PASSES * (work * 20 + 6 * full * CPAD * CPAD * LANES),
            bytes_accessed=4 * (work + rows * chans * cols),
            transcendentals=0,
        ),
    )(field, ew, top, bot, lvl, bal_t)


def local(innovations, owner_tile, obs_column, obs_depth, coefficients, sea_depth, balance):
    channels = innovations.shape[0]
    obs_count = innovations.shape[1]
    devices = lax.axis_size("lon") * lax.axis_size("lat")
    capacity = 4 * obs_count // devices
    rows_y = sea_depth.shape[0]
    cols_x = sea_depth.shape[1]

    stat = jnp.concatenate([coefficients, sea_depth.astype(jnp.float32)[None]], axis=0)
    stat = jnp.transpose(stat, (1, 2, 0)).reshape(rows_y * cols_x, stat.shape[0])
    base = jnp.concatenate(
        [
            jnp.zeros((rows_y * cols_x, CPAD), jnp.float32),
            stat,
            jnp.zeros((rows_y * cols_x, SPAD - stat.shape[1]), jnp.float32),
        ],
        axis=1,
    )

    level_ids = jnp.arange(channels) % LEVELS
    kept = jnp.where(level_ids[:, None] < obs_depth[None, :], innovations, 0.0)
    targets = owner_tile[:, 0]
    one_hot = (targets[:, None] == jnp.arange(devices, dtype=jnp.int32)[None, :]).astype(jnp.int32)
    before = jnp.cumsum(one_hot, axis=0) - one_hot
    slot_rank = jnp.sum(before * one_hot, axis=1)
    destination = targets * capacity + slot_rank
    payload = jnp.concatenate(
        [
            kept.T,
            jnp.zeros((obs_count, CPAD - channels - 1), jnp.float32),
            obs_column.astype(jnp.float32)[:, None],
        ],
        axis=1,
    )
    send = jnp.zeros((devices * capacity, CPAD), jnp.float32).at[destination].set(payload)
    got = lax.all_to_all(
        send.reshape(devices, capacity, CPAD), ("lon", "lat"), 0, 0, tiled=True
    ).reshape(devices * capacity, CPAD)
    where = got[:, CPAD - 1].astype(jnp.int32)
    got = jnp.pad(got, ((0, 0), (0, SPAD)))
    field = base.at[where].add(got)
    field = field.reshape(rows_y, cols_x, CPAD + SPAD)
    out = run_passes(field, field_halos(field), balance, channels)
    return jnp.transpose(out, (1, 0, 2))


def solution(mesh):
    placed = (
        P(None, ("lon", "lat")),
        P(("lon", "lat"), None),
        P(("lon", "lat")),
        P(("lon", "lat")),
        P(None, "lat", "lon"),
        P("lat", "lon"),
        P(),
    )
    return jax.shard_map(
        local, mesh=mesh, in_specs=placed, out_specs=P(None, "lat", "lon"), check_vma=False
    )
```

```python
import jax
import jax.numpy as jnp
from jax import lax
from jax.experimental import pallas as pl
from jax.experimental.pallas import tpu as pltpu
from jax.sharding import PartitionSpec as P

LEVELS = 75
PASSES = 4
RADIUS = PASSES
LANES = 256
CPAD = 152
CHUNK = 8
SPAD = 16


def shift_lon(block, step):
    count = lax.axis_size("lon")
    return lax.ppermute(block, "lon", [(i, (i + step) % count) for i in range(count)])


def shift_lat(block, step):
    count = lax.axis_size("lat")
    return lax.ppermute(
        block, "lat", [(i, i + step) for i in range(count) if 0 <= i + step < count]
    )


def shift_both(block, step_lon, step_lat):
    n_lon = lax.axis_size("lon")
    n_lat = lax.axis_size("lat")
    pairs = []
    for i in range(n_lon):
        for j in range(n_lat):
            if 0 <= j + step_lat < n_lat:
                pairs.append((i * n_lat + j, ((i + step_lon) % n_lon) * n_lat + j + step_lat))
    return lax.ppermute(block, ("lon", "lat"), pairs)


DIRECTIONS = (
    ("west", lambda v, r: v[:, :, v.shape[2] - r :], "lon", 1, 0),
    ("east", lambda v, r: v[:, :, :r], "lon", -1, 0),
    ("south", lambda v, r: v[v.shape[0] - r :], "lat", 0, 1),
    ("north", lambda v, r: v[:r], "lat", 0, -1),
    ("sw", lambda v, r: v[v.shape[0] - r :, :, v.shape[2] - r :], "both", 1, 1),
    ("se", lambda v, r: v[v.shape[0] - r :, :, :r], "both", -1, 1),
    ("nw", lambda v, r: v[:r, :, v.shape[2] - r :], "both", 1, -1),
    ("ne", lambda v, r: v[:r, :, :r], "both", -1, -1),
)


def exchange(parts):
    got = [dict() for _ in parts]
    for name, take, axis, step_lon, step_lat in DIRECTIONS:
        pieces = [take(v, RADIUS) for v in parts]
        flat = jnp.concatenate([p.reshape(-1) for p in pieces])
        if axis == "lon":
            flat = shift_lon(flat, step_lon)
        elif axis == "lat":
            flat = shift_lat(flat, step_lat)
        else:
            flat = shift_both(flat, step_lon, step_lat)
        offset = 0
        for i, p in enumerate(pieces):
            got[i][name] = flat[offset : offset + p.size].reshape(p.shape)
            offset += p.size
    return got


def field_halos(f):
    rows, cols, _ = f.shape
    r = RADIUS
    v_top = jnp.transpose(f[:r], (0, 2, 1))
    v_bot = jnp.transpose(f[rows - r :], (0, 2, 1))

    def t(a):
        return jnp.transpose(a, (0, 2, 1))

    return {
        "west": shift_lon(f[:, cols - r :, :], 1),
        "east": shift_lon(f[:, :r, :], -1),
        "south": shift_lat(v_bot, 1),
        "north": shift_lat(v_top, -1),
        "sw": t(shift_both(f[rows - r :, cols - r :, :], 1, 1)),
        "se": t(shift_both(f[rows - r :, :r, :], -1, 1)),
        "nw": t(shift_both(f[:r, cols - r :, :], 1, -1)),
        "ne": t(shift_both(f[:r, :r, :], -1, -1)),
    }


def side_lanes(east, west, gap):
    zeros = jnp.zeros(east.shape[:2] + (gap,), jnp.float32)
    return jnp.concatenate([east, zeros, west], axis=2)


def assemble(v, h):
    cols = v.shape[2]
    gap = LANES - cols - 2 * RADIUS
    top = jnp.concatenate([h["south"], side_lanes(h["se"], h["sw"], gap)], axis=2)
    mid = jnp.concatenate([v, side_lanes(h["east"], h["west"], gap)], axis=2)
    bot = jnp.concatenate([h["north"], side_lanes(h["ne"], h["nw"], gap)], axis=2)
    return jnp.concatenate([top, mid, bot], axis=0)


def split_bf16(x):
    hi = x.astype(jnp.bfloat16)
    lo = (x - hi.astype(jnp.float32)).astype(jnp.bfloat16)
    return hi, lo


def passes_kernel(
    v_ref, ew_ref, top_ref, bot_ref, lvl_ref, bal_ref, out_ref, a_ref, b_ref, p_ref, s_ref, u_ref
):
    full = p_ref.shape[0]
    rows = v_ref.shape[0]
    cols = v_ref.shape[1]
    chans = p_ref.shape[1]
    out_ch = out_ref.shape[1]
    statc = s_ref.shape[1]
    p_ref[:RADIUS] = top_ref[:, :chans, :]
    s_ref[:RADIUS] = top_ref[:, chans:, :]
    p_ref[full - RADIUS :] = bot_ref[:, :chans, :]
    s_ref[full - RADIUS :] = bot_ref[:, chans:, :]

    def fill(y, carry):
        body = jnp.transpose(v_ref[y])
        sides = jnp.transpose(ew_ref[y])
        for ref, lo, n in ((p_ref, 0, chans), (s_ref, chans, statc)):
            ref[y + RADIUS, :, :cols] = body[lo : lo + n]
            ref[y + RADIUS, :, cols:] = jnp.zeros((n, LANES - cols), jnp.float32)
            ref[y + RADIUS, :, cols : cols + RADIUS] = sides[lo : lo + n, :RADIUS]
            ref[y + RADIUS, :, LANES - RADIUS :] = sides[lo : lo + n, RADIUS:]
        return carry

    lax.fori_loop(0, rows, fill, 0, unroll=4)
    b_hi, b_lo = split_bf16(bal_ref[...])
    srcs = [p_ref, a_ref, b_ref, a_ref]
    dsts = [a_ref, b_ref, a_ref, None]
    for p in range(PASSES):
        src = srcs[p]
        dst = dsts[p]

        def row(y, carry, src=src, dst=dst):
            srows = [s_ref[y - dy] for dy in (-1, 0, 1)]
            coefs = {}
            for dy in (-1, 0, 1):
                for dx in (-1, 0, 1):
                    k = (dy + 1) * 3 + dx + 1
                    coefs[(dy, dx)] = jnp.broadcast_to(
                        srows[dy + 1][k : k + 1, :], (CHUNK, LANES)
                    )
            depth = jnp.broadcast_to(srows[1][9:10, :], (CHUNK, LANES))
            for c0 in range(0, chans, CHUNK):
                sums = [None, None, None]
                for dy in (-1, 0, 1):
                    v = src[y - dy, c0 : c0 + CHUNK, :]
                    for dx in (-1, 0, 1):
                        t = coefs[(dy, dx)] * v
                        sums[dx + 1] = t if sums[dx + 1] is None else sums[dx + 1] + t
                acc = (
                    sums[1]
                    + pltpu.roll(sums[0], LANES - 1, 1)
                    + pltpu.roll(sums[2], 1, 1)
                )
                u_ref[c0 : c0 + CHUNK, :] = jnp.where(
                    lvl_ref[c0 : c0 + CHUNK, :] < depth, acc, 0.0
                )
            u_hi, u_lo = split_bf16(u_ref[...])
            res = jnp.dot(b_hi, u_hi, preferred_element_type=jnp.float32)
            res = res + jnp.dot(b_hi, u_lo, preferred_element_type=jnp.float32)
            res = res + jnp.dot(b_lo, u_hi, preferred_element_type=jnp.float32)
            if dst is None:
                out_ref[y - RADIUS] = res[:out_ch, :cols]
            else:
                dst[y] = res
            return carry

        lax.fori_loop(p + 1, full - 1 - p, row, 0, unroll=16)


def run_passes(field, halos, balance, chans):
    rows, cols, cpad = field.shape
    full = rows + 2 * RADIUS
    gap = LANES - cols - 2 * RADIUS
    ew = jnp.concatenate([halos["east"], halos["west"]], axis=1)
    top = jnp.concatenate([halos["south"], side_lanes(halos["se"], halos["sw"], gap)], axis=2)
    bot = jnp.concatenate([halos["north"], side_lanes(halos["ne"], halos["nw"], gap)], axis=2)
    lvl = jnp.broadcast_to(
        (jnp.arange(CPAD) % LEVELS).astype(jnp.float32)[:, None], (CPAD, LANES)
    )
    bal_t = jnp.pad(balance.T, ((0, CPAD - chans), (0, CPAD - chans)))
    vmem = pltpu.VMEM
    work = full * CPAD * LANES
    return pl.pallas_call(
        passes_kernel,
        out_shape=jax.ShapeDtypeStruct((rows, chans, cols), jnp.float32),
        in_specs=[pl.BlockSpec(memory_space=vmem)] * 6,
        out_specs=pl.BlockSpec(memory_space=vmem),
        scratch_shapes=[
            vmem((full, CPAD, LANES), jnp.float32),
            vmem((full, CPAD, LANES), jnp.float32),
            vmem((full, CPAD, LANES), jnp.float32),
            vmem((full, SPAD, LANES), jnp.float32),
            vmem((CPAD, LANES), jnp.float32),
        ],
        compiler_params=pltpu.CompilerParams(vmem_limit_bytes=62 * 1024 * 1024),
        cost_estimate=pl.CostEstimate(
            flops=PASSES * (work * 20 + 6 * full * CPAD * CPAD * LANES),
            bytes_accessed=4 * (work + rows * chans * cols),
            transcendentals=0,
        ),
    )(field, ew, top, bot, lvl, bal_t)


def local(innovations, owner_tile, obs_column, obs_depth, coefficients, sea_depth, balance):
    channels = innovations.shape[0]
    obs_count = innovations.shape[1]
    devices = lax.axis_size("lon") * lax.axis_size("lat")
    capacity = 4 * obs_count // devices
    rows_y = sea_depth.shape[0]
    cols_x = sea_depth.shape[1]

    stat = jnp.concatenate([coefficients, sea_depth.astype(jnp.float32)[None]], axis=0)
    stat = jnp.transpose(stat, (1, 2, 0)).reshape(rows_y * cols_x, stat.shape[0])
    base = jnp.concatenate(
        [
            jnp.zeros((rows_y * cols_x, CPAD), jnp.float32),
            stat,
            jnp.zeros((rows_y * cols_x, SPAD - stat.shape[1]), jnp.float32),
        ],
        axis=1,
    )

    level_ids = jnp.arange(channels) % LEVELS
    kept = jnp.where(level_ids[:, None] < obs_depth[None, :], innovations, 0.0)
    targets = owner_tile[:, 0]
    one_hot = (targets[:, None] == jnp.arange(devices, dtype=jnp.int32)[None, :]).astype(jnp.int32)
    before = jnp.cumsum(one_hot, axis=0) - one_hot
    slot_rank = jnp.sum(before * one_hot, axis=1)
    destination = targets * capacity + slot_rank
    payload = jnp.concatenate(
        [
            kept.T,
            jnp.zeros((obs_count, CPAD - channels - 1), jnp.float32),
            obs_column.astype(jnp.float32)[:, None],
        ],
        axis=1,
    )
    send = jnp.zeros((devices * capacity, CPAD), jnp.float32).at[destination].set(payload)
    got = lax.all_to_all(
        send.reshape(devices, capacity, CPAD), ("lon", "lat"), 0, 0, tiled=True
    ).reshape(devices * capacity, CPAD)
    where = got[:, CPAD - 1].astype(jnp.int32)
    got = jnp.pad(got, ((0, 0), (0, SPAD)))
    field = base.at[where].add(got)
    field = field.reshape(rows_y, cols_x, CPAD + SPAD)
    out = run_passes(field, field_halos(field), balance, channels)
    return jnp.transpose(out, (1, 0, 2))


def solution(mesh):
    placed = (
        P(None, ("lon", "lat")),
        P(("lon", "lat"), None),
        P(("lon", "lat")),
        P(("lon", "lat")),
        P(None, "lat", "lon"),
        P("lat", "lon"),
        P(),
    )
    return jax.shard_map(
        local, mesh=mesh, in_specs=placed, out_specs=P(None, "lat", "lon"), check_vma=False
    )
```

```python
import jax
import jax.numpy as jnp
from jax import lax
from jax.experimental import pallas as pl
from jax.experimental.pallas import tpu as pltpu
from jax.sharding import PartitionSpec as P

LEVELS = 75
PASSES = 4
RADIUS = PASSES
LANES = 256
CPAD = 152
CHUNK = 8
SPAD = 16


def shift_lon(block, step):
    count = lax.axis_size("lon")
    return lax.ppermute(block, "lon", [(i, (i + step) % count) for i in range(count)])


def shift_lat(block, step):
    count = lax.axis_size("lat")
    return lax.ppermute(
        block, "lat", [(i, i + step) for i in range(count) if 0 <= i + step < count]
    )


def shift_both(block, step_lon, step_lat):
    n_lon = lax.axis_size("lon")
    n_lat = lax.axis_size("lat")
    pairs = []
    for i in range(n_lon):
        for j in range(n_lat):
            if 0 <= j + step_lat < n_lat:
                pairs.append((i * n_lat + j, ((i + step_lon) % n_lon) * n_lat + j + step_lat))
    return lax.ppermute(block, ("lon", "lat"), pairs)


DIRECTIONS = (
    ("west", lambda v, r: v[:, :, v.shape[2] - r :], "lon", 1, 0),
    ("east", lambda v, r: v[:, :, :r], "lon", -1, 0),
    ("south", lambda v, r: v[v.shape[0] - r :], "lat", 0, 1),
    ("north", lambda v, r: v[:r], "lat", 0, -1),
    ("sw", lambda v, r: v[v.shape[0] - r :, :, v.shape[2] - r :], "both", 1, 1),
    ("se", lambda v, r: v[v.shape[0] - r :, :, :r], "both", -1, 1),
    ("nw", lambda v, r: v[:r, :, v.shape[2] - r :], "both", 1, -1),
    ("ne", lambda v, r: v[:r, :, :r], "both", -1, -1),
)


def exchange(parts):
    got = [dict() for _ in parts]
    for name, take, axis, step_lon, step_lat in DIRECTIONS:
        pieces = [take(v, RADIUS) for v in parts]
        flat = jnp.concatenate([p.reshape(-1) for p in pieces])
        if axis == "lon":
            flat = shift_lon(flat, step_lon)
        elif axis == "lat":
            flat = shift_lat(flat, step_lat)
        else:
            flat = shift_both(flat, step_lon, step_lat)
        offset = 0
        for i, p in enumerate(pieces):
            got[i][name] = flat[offset : offset + p.size].reshape(p.shape)
            offset += p.size
    return got


def field_halos(f):
    rows, cols, _ = f.shape
    r = RADIUS
    v_top = jnp.transpose(f[:r], (0, 2, 1))
    v_bot = jnp.transpose(f[rows - r :], (0, 2, 1))

    def t(a):
        return jnp.transpose(a, (0, 2, 1))

    return {
        "west": shift_lon(f[:, cols - r :, :], 1),
        "east": shift_lon(f[:, :r, :], -1),
        "south": shift_lat(v_bot, 1),
        "north": shift_lat(v_top, -1),
        "sw": t(shift_both(f[rows - r :, cols - r :, :], 1, 1)),
        "se": t(shift_both(f[rows - r :, :r, :], -1, 1)),
        "nw": t(shift_both(f[:r, cols - r :, :], 1, -1)),
        "ne": t(shift_both(f[:r, :r, :], -1, -1)),
    }


def side_lanes(east, west, gap):
    zeros = jnp.zeros(east.shape[:2] + (gap,), jnp.float32)
    return jnp.concatenate([east, zeros, west], axis=2)


def assemble(v, h):
    cols = v.shape[2]
    gap = LANES - cols - 2 * RADIUS
    top = jnp.concatenate([h["south"], side_lanes(h["se"], h["sw"], gap)], axis=2)
    mid = jnp.concatenate([v, side_lanes(h["east"], h["west"], gap)], axis=2)
    bot = jnp.concatenate([h["north"], side_lanes(h["ne"], h["nw"], gap)], axis=2)
    return jnp.concatenate([top, mid, bot], axis=0)


def split_bf16(x):
    hi = x.astype(jnp.bfloat16)
    lo = (x - hi.astype(jnp.float32)).astype(jnp.bfloat16)
    return hi, lo


def passes_kernel(
    v_ref, ew_ref, top_ref, bot_ref, lvl_ref, bal_ref, out_ref, a_ref, b_ref, p_ref, s_ref, u_ref
):
    full = p_ref.shape[0]
    rows = v_ref.shape[0]
    cols = v_ref.shape[1]
    chans = p_ref.shape[1]
    out_ch = out_ref.shape[1]
    statc = s_ref.shape[1]
    p_ref[:RADIUS] = top_ref[:, :chans, :]
    s_ref[:RADIUS] = top_ref[:, chans:, :]
    p_ref[full - RADIUS :] = bot_ref[:, :chans, :]
    s_ref[full - RADIUS :] = bot_ref[:, chans:, :]

    def fill(y, carry):
        body = jnp.transpose(v_ref[y])
        sides = jnp.transpose(ew_ref[y])
        for ref, lo, n in ((p_ref, 0, chans), (s_ref, chans, statc)):
            ref[y + RADIUS, :, :cols] = body[lo : lo + n]
            ref[y + RADIUS, :, cols:] = jnp.zeros((n, LANES - cols), jnp.float32)
            ref[y + RADIUS, :, cols : cols + RADIUS] = sides[lo : lo + n, :RADIUS]
            ref[y + RADIUS, :, LANES - RADIUS :] = sides[lo : lo + n, RADIUS:]
        return carry

    lax.fori_loop(0, rows, fill, 0, unroll=4)
    b_hi, b_lo = split_bf16(bal_ref[...])
    srcs = [p_ref, a_ref, b_ref, a_ref]
    dsts = [a_ref, b_ref, a_ref, None]
    for p in range(PASSES):
        src = srcs[p]
        dst = dsts[p]

        def row(y, carry, src=src, dst=dst):
            srows = [s_ref[y - dy] for dy in (-1, 0, 1)]
            coefs = {}
            for dy in (-1, 0, 1):
                for dx in (-1, 0, 1):
                    k = (dy + 1) * 3 + dx + 1
                    coefs[(dy, dx)] = jnp.broadcast_to(
                        srows[dy + 1][k : k + 1, :], (CHUNK, LANES)
                    )
            depth = jnp.broadcast_to(srows[1][9:10, :], (CHUNK, LANES))
            for c0 in range(0, chans, CHUNK):
                sums = [None, None, None]
                for dy in (-1, 0, 1):
                    v = src[y - dy, c0 : c0 + CHUNK, :]
                    for dx in (-1, 0, 1):
                        t = coefs[(dy, dx)] * v
                        sums[dx + 1] = t if sums[dx + 1] is None else sums[dx + 1] + t
                acc = (
                    sums[1]
                    + pltpu.roll(sums[0], LANES - 1, 1)
                    + pltpu.roll(sums[2], 1, 1)
                )
                u_ref[c0 : c0 + CHUNK, :] = jnp.where(
                    lvl_ref[c0 : c0 + CHUNK, :] < depth, acc, 0.0
                )
            u_hi, u_lo = split_bf16(u_ref[...])
            res = jnp.dot(b_hi, u_hi, preferred_element_type=jnp.float32)
            res = res + jnp.dot(b_hi, u_lo, preferred_element_type=jnp.float32)
            res = res + jnp.dot(b_lo, u_hi, preferred_element_type=jnp.float32)
            if dst is None:
                out_ref[y - RADIUS] = res[:out_ch, :cols]
            else:
                dst[y] = res
            return carry

        count = full - 2 - 2 * p
        unroll = max(d for d in range(1, 18) if count % d == 0)
        lax.fori_loop(p + 1, full - 1 - p, row, 0, unroll=unroll)


def run_passes(field, halos, balance, chans):
    rows, cols, cpad = field.shape
    full = rows + 2 * RADIUS
    gap = LANES - cols - 2 * RADIUS
    ew = jnp.concatenate([halos["east"], halos["west"]], axis=1)
    top = jnp.concatenate([halos["south"], side_lanes(halos["se"], halos["sw"], gap)], axis=2)
    bot = jnp.concatenate([halos["north"], side_lanes(halos["ne"], halos["nw"], gap)], axis=2)
    lvl = jnp.broadcast_to(
        (jnp.arange(CPAD) % LEVELS).astype(jnp.float32)[:, None], (CPAD, LANES)
    )
    bal_t = jnp.pad(balance.T, ((0, CPAD - chans), (0, CPAD - chans)))
    vmem = pltpu.VMEM
    work = full * CPAD * LANES
    return pl.pallas_call(
        passes_kernel,
        out_shape=jax.ShapeDtypeStruct((rows, chans, cols), jnp.float32),
        in_specs=[pl.BlockSpec(memory_space=vmem)] * 6,
        out_specs=pl.BlockSpec(memory_space=vmem),
        scratch_shapes=[
            vmem((full, CPAD, LANES), jnp.float32),
            vmem((full, CPAD, LANES), jnp.float32),
            vmem((full, CPAD, LANES), jnp.float32),
            vmem((full, SPAD, LANES), jnp.float32),
            vmem((CPAD, LANES), jnp.float32),
        ],
        compiler_params=pltpu.CompilerParams(vmem_limit_bytes=62 * 1024 * 1024),
        cost_estimate=pl.CostEstimate(
            flops=PASSES * (work * 20 + 6 * full * CPAD * CPAD * LANES),
            bytes_accessed=4 * (work + rows * chans * cols),
            transcendentals=0,
        ),
    )(field, ew, top, bot, lvl, bal_t)


def local(innovations, owner_tile, obs_column, obs_depth, coefficients, sea_depth, balance):
    channels = innovations.shape[0]
    obs_count = innovations.shape[1]
    devices = lax.axis_size("lon") * lax.axis_size("lat")
    capacity = 4 * obs_count // devices
    rows_y = sea_depth.shape[0]
    cols_x = sea_depth.shape[1]

    stat = jnp.concatenate([coefficients, sea_depth.astype(jnp.float32)[None]], axis=0)
    stat = jnp.transpose(stat, (1, 2, 0)).reshape(rows_y * cols_x, stat.shape[0])
    base = jnp.concatenate(
        [
            jnp.zeros((rows_y * cols_x, CPAD), jnp.float32),
            stat,
            jnp.zeros((rows_y * cols_x, SPAD - stat.shape[1]), jnp.float32),
        ],
        axis=1,
    )

    level_ids = jnp.arange(channels) % LEVELS
    kept = jnp.where(level_ids[:, None] < obs_depth[None, :], innovations, 0.0)
    targets = owner_tile[:, 0]
    one_hot = (targets[:, None] == jnp.arange(devices, dtype=jnp.int32)[None, :]).astype(jnp.int32)
    before = jnp.cumsum(one_hot, axis=0) - one_hot
    slot_rank = jnp.sum(before * one_hot, axis=1)
    destination = targets * capacity + slot_rank
    payload = jnp.concatenate(
        [
            kept.T,
            jnp.zeros((obs_count, CPAD - channels - 1), jnp.float32),
            obs_column.astype(jnp.float32)[:, None],
        ],
        axis=1,
    )
    send = jnp.zeros((devices * capacity, CPAD), jnp.float32).at[destination].set(payload)
    got = lax.all_to_all(
        send.reshape(devices, capacity, CPAD), ("lon", "lat"), 0, 0, tiled=True
    ).reshape(devices * capacity, CPAD)
    where = got[:, CPAD - 1].astype(jnp.int32)
    got = jnp.pad(got, ((0, 0), (0, SPAD)))
    field = base.at[where].add(got)
    field = field.reshape(rows_y, cols_x, CPAD + SPAD)
    out = run_passes(field, field_halos(field), balance, channels)
    return jnp.transpose(out, (1, 0, 2))


def solution(mesh):
    placed = (
        P(None, ("lon", "lat")),
        P(("lon", "lat"), None),
        P(("lon", "lat")),
        P(("lon", "lat")),
        P(None, "lat", "lon"),
        P("lat", "lon"),
        P(),
    )
    return jax.shard_map(
        local, mesh=mesh, in_specs=placed, out_specs=P(None, "lat", "lon"), check_vma=False
    )
```

```python
import jax
import jax.numpy as jnp
from jax import lax
from jax.experimental import pallas as pl
from jax.experimental.pallas import tpu as pltpu
from jax.sharding import PartitionSpec as P

LEVELS = 75
PASSES = 4
RADIUS = PASSES
LANES = 256
CPAD = 152
CHUNK = 8
SPAD = 16


def shift_lon(block, step):
    count = lax.axis_size("lon")
    return lax.ppermute(block, "lon", [(i, (i + step) % count) for i in range(count)])


def shift_lat(block, step):
    count = lax.axis_size("lat")
    return lax.ppermute(
        block, "lat", [(i, i + step) for i in range(count) if 0 <= i + step < count]
    )


def shift_both(block, step_lon, step_lat):
    n_lon = lax.axis_size("lon")
    n_lat = lax.axis_size("lat")
    pairs = []
    for i in range(n_lon):
        for j in range(n_lat):
            if 0 <= j + step_lat < n_lat:
                pairs.append((i * n_lat + j, ((i + step_lon) % n_lon) * n_lat + j + step_lat))
    return lax.ppermute(block, ("lon", "lat"), pairs)


DIRECTIONS = (
    ("west", lambda v, r: v[:, :, v.shape[2] - r :], "lon", 1, 0),
    ("east", lambda v, r: v[:, :, :r], "lon", -1, 0),
    ("south", lambda v, r: v[v.shape[0] - r :], "lat", 0, 1),
    ("north", lambda v, r: v[:r], "lat", 0, -1),
    ("sw", lambda v, r: v[v.shape[0] - r :, :, v.shape[2] - r :], "both", 1, 1),
    ("se", lambda v, r: v[v.shape[0] - r :, :, :r], "both", -1, 1),
    ("nw", lambda v, r: v[:r, :, v.shape[2] - r :], "both", 1, -1),
    ("ne", lambda v, r: v[:r, :, :r], "both", -1, -1),
)


def exchange(parts):
    got = [dict() for _ in parts]
    for name, take, axis, step_lon, step_lat in DIRECTIONS:
        pieces = [take(v, RADIUS) for v in parts]
        flat = jnp.concatenate([p.reshape(-1) for p in pieces])
        if axis == "lon":
            flat = shift_lon(flat, step_lon)
        elif axis == "lat":
            flat = shift_lat(flat, step_lat)
        else:
            flat = shift_both(flat, step_lon, step_lat)
        offset = 0
        for i, p in enumerate(pieces):
            got[i][name] = flat[offset : offset + p.size].reshape(p.shape)
            offset += p.size
    return got


def field_halos(f):
    rows, cols, _ = f.shape
    r = RADIUS
    v_top = jnp.transpose(f[:r], (0, 2, 1))
    v_bot = jnp.transpose(f[rows - r :], (0, 2, 1))

    def t(a):
        return jnp.transpose(a, (0, 2, 1))

    return {
        "west": shift_lon(f[:, cols - r :, :], 1),
        "east": shift_lon(f[:, :r, :], -1),
        "south": shift_lat(v_bot, 1),
        "north": shift_lat(v_top, -1),
        "sw": t(shift_both(f[rows - r :, cols - r :, :], 1, 1)),
        "se": t(shift_both(f[rows - r :, :r, :], -1, 1)),
        "nw": t(shift_both(f[:r, cols - r :, :], 1, -1)),
        "ne": t(shift_both(f[:r, :r, :], -1, -1)),
    }


def side_lanes(east, west, gap):
    zeros = jnp.zeros(east.shape[:2] + (gap,), jnp.float32)
    return jnp.concatenate([east, zeros, west], axis=2)


def assemble(v, h):
    cols = v.shape[2]
    gap = LANES - cols - 2 * RADIUS
    top = jnp.concatenate([h["south"], side_lanes(h["se"], h["sw"], gap)], axis=2)
    mid = jnp.concatenate([v, side_lanes(h["east"], h["west"], gap)], axis=2)
    bot = jnp.concatenate([h["north"], side_lanes(h["ne"], h["nw"], gap)], axis=2)
    return jnp.concatenate([top, mid, bot], axis=0)


def split_bf16(x):
    hi = x.astype(jnp.bfloat16)
    lo = (x - hi.astype(jnp.float32)).astype(jnp.bfloat16)
    return hi, lo


def passes_kernel(
    v_ref, ew_ref, top_ref, bot_ref, lvl_ref, bal_ref, out_ref, a_ref, b_ref, p_ref, s_ref, u_ref
):
    full = p_ref.shape[0]
    rows = v_ref.shape[0]
    cols = v_ref.shape[1]
    chans = p_ref.shape[1]
    out_ch = out_ref.shape[1]
    statc = s_ref.shape[1]
    p_ref[:RADIUS] = top_ref[:, :chans, :]
    s_ref[:RADIUS] = top_ref[:, chans:, :]
    p_ref[full - RADIUS :] = bot_ref[:, :chans, :]
    s_ref[full - RADIUS :] = bot_ref[:, chans:, :]

    def fill(y, carry):
        body = jnp.transpose(v_ref[y])
        sides = jnp.transpose(ew_ref[y])
        for ref, lo, n in ((p_ref, 0, chans), (s_ref, chans, statc)):
            ref[y + RADIUS, :, :cols] = body[lo : lo + n]
            ref[y + RADIUS, :, cols:] = jnp.zeros((n, LANES - cols), jnp.float32)
            ref[y + RADIUS, :, cols : cols + RADIUS] = sides[lo : lo + n, :RADIUS]
            ref[y + RADIUS, :, LANES - RADIUS :] = sides[lo : lo + n, RADIUS:]
        return carry

    lax.fori_loop(0, rows, fill, 0, unroll=8)
    b_hi, b_lo = split_bf16(bal_ref[...])
    srcs = [p_ref, a_ref, b_ref, a_ref]
    dsts = [a_ref, b_ref, a_ref, None]
    for p in range(PASSES):
        src = srcs[p]
        dst = dsts[p]

        def row(y, carry, src=src, dst=dst):
            srows = [s_ref[y - dy] for dy in (-1, 0, 1)]
            coefs = {}
            for dy in (-1, 0, 1):
                for dx in (-1, 0, 1):
                    k = (dy + 1) * 3 + dx + 1
                    coefs[(dy, dx)] = jnp.broadcast_to(
                        srows[dy + 1][k : k + 1, :], (CHUNK, LANES)
                    )
            depth = jnp.broadcast_to(srows[1][9:10, :], (CHUNK, LANES))
            for c0 in range(0, chans, CHUNK):
                sums = [None, None, None]
                for dy in (-1, 0, 1):
                    v = src[y - dy, c0 : c0 + CHUNK, :]
                    for dx in (-1, 0, 1):
                        t = coefs[(dy, dx)] * v
                        sums[dx + 1] = t if sums[dx + 1] is None else sums[dx + 1] + t
                acc = (
                    sums[1]
                    + pltpu.roll(sums[0], LANES - 1, 1)
                    + pltpu.roll(sums[2], 1, 1)
                )
                u_ref[c0 : c0 + CHUNK, :] = jnp.where(
                    lvl_ref[c0 : c0 + CHUNK, :] < depth, acc, 0.0
                )
            u_hi, u_lo = split_bf16(u_ref[...])
            res = jnp.dot(b_hi, u_hi, preferred_element_type=jnp.float32)
            res = res + jnp.dot(b_hi, u_lo, preferred_element_type=jnp.float32)
            res = res + jnp.dot(b_lo, u_hi, preferred_element_type=jnp.float32)
            if dst is None:
                out_ref[y - RADIUS] = res[:out_ch, :cols]
            else:
                dst[y] = res
            return carry

        count = full - 2 - 2 * p
        unroll = max(d for d in range(1, 18) if count % d == 0)
        lax.fori_loop(p + 1, full - 1 - p, row, 0, unroll=unroll)


def run_passes(field, halos, balance, chans):
    rows, cols, cpad = field.shape
    full = rows + 2 * RADIUS
    gap = LANES - cols - 2 * RADIUS
    ew = jnp.concatenate([halos["east"], halos["west"]], axis=1)
    top = jnp.concatenate([halos["south"], side_lanes(halos["se"], halos["sw"], gap)], axis=2)
    bot = jnp.concatenate([halos["north"], side_lanes(halos["ne"], halos["nw"], gap)], axis=2)
    lvl = jnp.broadcast_to(
        (jnp.arange(CPAD) % LEVELS).astype(jnp.float32)[:, None], (CPAD, LANES)
    )
    bal_t = jnp.pad(balance.T, ((0, CPAD - chans), (0, CPAD - chans)))
    vmem = pltpu.VMEM
    work = full * CPAD * LANES
    return pl.pallas_call(
        passes_kernel,
        out_shape=jax.ShapeDtypeStruct((rows, chans, cols), jnp.float32),
        in_specs=[pl.BlockSpec(memory_space=vmem)] * 6,
        out_specs=pl.BlockSpec(memory_space=vmem),
        scratch_shapes=[
            vmem((full, CPAD, LANES), jnp.float32),
            vmem((full, CPAD, LANES), jnp.float32),
            vmem((full, CPAD, LANES), jnp.float32),
            vmem((full, SPAD, LANES), jnp.float32),
            vmem((CPAD, LANES), jnp.float32),
        ],
        compiler_params=pltpu.CompilerParams(vmem_limit_bytes=62 * 1024 * 1024),
        cost_estimate=pl.CostEstimate(
            flops=PASSES * (work * 20 + 6 * full * CPAD * CPAD * LANES),
            bytes_accessed=4 * (work + rows * chans * cols),
            transcendentals=0,
        ),
    )(field, ew, top, bot, lvl, bal_t)


def local(innovations, owner_tile, obs_column, obs_depth, coefficients, sea_depth, balance):
    channels = innovations.shape[0]
    obs_count = innovations.shape[1]
    devices = lax.axis_size("lon") * lax.axis_size("lat")
    capacity = 4 * obs_count // devices
    rows_y = sea_depth.shape[0]
    cols_x = sea_depth.shape[1]

    stat = jnp.concatenate([coefficients, sea_depth.astype(jnp.float32)[None]], axis=0)
    stat = jnp.transpose(stat, (1, 2, 0)).reshape(rows_y * cols_x, stat.shape[0])
    base = jnp.concatenate(
        [
            jnp.zeros((rows_y * cols_x, CPAD), jnp.float32),
            stat,
            jnp.zeros((rows_y * cols_x, SPAD - stat.shape[1]), jnp.float32),
        ],
        axis=1,
    )

    level_ids = jnp.arange(channels) % LEVELS
    kept = jnp.where(level_ids[:, None] < obs_depth[None, :], innovations, 0.0)
    targets = owner_tile[:, 0]
    one_hot = (targets[:, None] == jnp.arange(devices, dtype=jnp.int32)[None, :]).astype(jnp.int32)
    before = jnp.cumsum(one_hot, axis=0) - one_hot
    slot_rank = jnp.sum(before * one_hot, axis=1)
    destination = targets * capacity + slot_rank
    payload = jnp.concatenate(
        [
            kept.T,
            jnp.zeros((obs_count, CPAD - channels - 1), jnp.float32),
            obs_column.astype(jnp.float32)[:, None],
        ],
        axis=1,
    )
    send = jnp.zeros((devices * capacity, CPAD), jnp.float32).at[destination].set(payload)
    got = lax.all_to_all(
        send.reshape(devices, capacity, CPAD), ("lon", "lat"), 0, 0, tiled=True
    ).reshape(devices * capacity, CPAD)
    where = got[:, CPAD - 1].astype(jnp.int32)
    got = jnp.pad(got, ((0, 0), (0, SPAD)))
    field = base.at[where].add(got)
    field = field.reshape(rows_y, cols_x, CPAD + SPAD)
    out = run_passes(field, field_halos(field), balance, channels)
    return jnp.transpose(out, (1, 0, 2))


def solution(mesh):
    placed = (
        P(None, ("lon", "lat")),
        P(("lon", "lat"), None),
        P(("lon", "lat")),
        P(("lon", "lat")),
        P(None, "lat", "lon"),
        P("lat", "lon"),
        P(),
    )
    return jax.shard_map(
        local, mesh=mesh, in_specs=placed, out_specs=P(None, "lat", "lon"), check_vma=False
    )
```
